256 devices in a mesh: tp: 8 (over x, core), ha: 8 (over y, z_lo), wa: 4 (over z_hi).
Axes of the slice: x: 4, y: 4, z: 8 (z_hi: 4, z_lo: 2; z = z_hi * 2 + z_lo), core: 2. Of those that a mesh axis runs over, the one named last changes fastest.
Arguments:
- queries: bfloat16 [1, 16, 8, 128, 3072], P(None, 'ha', 'wa', None, 'tp'), may hold values from -128 to 128
- keys: bfloat16 [1, 16, 8, 128, 3072], P(None, 'ha', 'wa', None, 'tp'), may hold values from -4.5 to 4.5
- values: bfloat16 [1, 16, 8, 128, 3072], P(None, 'ha', 'wa', None, 'tp'), may hold values from -6 to 6
- grad_out: bfloat16 [1, 16, 8, 128, 3072], P(None, 'ha', 'wa', None, 'tp'), may hold values from -6 to 6
- out_proj: bfloat16 [3072, 3072], P(('ha', 'wa'), 'tp'), may hold values from -0.109375 to 0.109375
Outputs:
- grad_queries: bfloat16 [1, 16, 8, 128, 3072], P(None, 'ha', 'wa', None, 'tp')
- grad_keys: bfloat16 [1, 16, 8, 128, 3072], P(None, 'ha', 'wa', None, 'tp')
- grad_values: bfloat16 [1, 16, 8, 128, 3072], P(None, 'ha', 'wa', None, 'tp')
The draws below stay inside these ranges and needn't reach their ends.
All inputs are finite; a program needn't handle non-finite values.
Results may differ from the reference program's by a relative error of at most 0.014.
Values may be sent and summed in bfloat16 or wider, within the bound.
No kernel may reach another device: no remote copies, remote signals or barrier semaphores. Data moves between devices by JAX's collectives and lax.ppermute only.
A program may use at most 128 MiB of HBM per device.

```python
import jax
import jax.numpy as jnp
from jax import lax

D = 3072
HEADS = 24
HEAD = 128
TILE = 128
TF = 1
HD = 3072
NTH = 16
NTW = 8


def shared_keys(key):
    base = jax.random.normal(jax.random.fold_in(key, 7), (TF, NTH, NTW, TILE, HEADS * HEAD), jnp.float32)
    base = jnp.clip(base, -4.0, 4.0)
    return base


def draw_keys(key, part):
    return shared_keys(key).astype(jnp.bfloat16)


def draw_queries(key, part):
    base = jax.random.normal(jax.random.fold_in(key, 11), (TF, NTH, NTW, TILE, HEADS * HEAD), jnp.float32)
    base = jnp.clip(base, -4.0, 4.0)
    return base.astype(jnp.bfloat16)


def block_levels(own_key, shape, shards, low, largest):
    gain, own = 1.0, jax.random.fold_in(own_key, 6)
    for dim, shards_of in shards:
        draws = jnp.exp(jax.random.uniform(jax.random.fold_in(own, dim), (shards_of,), jnp.float32, low / len(shards), largest / len(shards)))
        gain = gain * jnp.repeat(draws, shape[dim] // shards_of).reshape([-1 if axis == dim else 1 for axis in range(len(shape))])
    return gain


def centred(rng, dims, deviation, most, cuts=(), kind=jnp.bfloat16):
    entries = deviation * jax.random.normal(rng, dims, jnp.float32)
    if cuts:
        entries = entries * block_levels(rng, dims, cuts, -0.22, 0.18)
    return jnp.clip(entries, -most, most).astype(kind)


def setup_inputs(seed: int = 0) -> dict:
    seeds = jax.random.split(jax.random.key(seed), 6)
    return {
        "queries": draw_queries(jax.random.fold_in(seeds[5], 71), 0),
        "keys": draw_keys(jax.random.fold_in(seeds[5], 71), 0),
        "values": centred(seeds[2], (TF, NTH, NTW, TILE, HD), 1.0, 6.0, ((1, 8), (2, 4), (4, 8))),
        "grad_out": centred(seeds[3], (TF, NTH, NTW, TILE, D), 1.0, 6.0, ((1, 8), (2, 4), (4, 8))),
        "out_proj": centred(seeds[4], (D, HD), D ** -0.5, 0.109375, ((0, 32), (1, 8))),
    }


def tile_backward(query_blk, key_blk, value_blk, grad_blk, softmax_scale):
    f32 = jnp.float32
    scores = jnp.einsum('qtd,qld->qtl', query_blk.astype(f32), key_blk.astype(f32)) * softmax_scale
    scores = scores - jnp.max(scores, axis=-1, keepdims=True)
    expo = jnp.exp(scores)
    probs = expo / jnp.sum(expo, axis=-1, keepdims=True)
    probs_lo = probs.astype(jnp.bfloat16)
    attn = jnp.einsum('qtl,qld->qtd', probs_lo.astype(f32), value_blk.astype(f32))
    delta = jnp.sum(grad_blk.astype(f32) * attn, axis=-1, keepdims=True)
    grad_probs = jnp.einsum('qtd,qld->qtl', grad_blk.astype(f32), value_blk.astype(f32))
    grad_scores = (probs * (grad_probs - delta) * softmax_scale).astype(jnp.bfloat16)
    grad_query = jnp.einsum('qtl,qld->qtd', grad_scores.astype(f32), key_blk.astype(f32))
    grad_key = jnp.einsum('qtl,qtd->qld', grad_scores.astype(f32), query_blk.astype(f32))
    grad_value = jnp.einsum('qtl,qtd->qld', probs_lo.astype(f32), grad_blk.astype(f32))
    return grad_query, grad_key, grad_value


def reference(queries, keys, values, grad_out, out_proj):
    frames, tile_rows, tile_cols, tile_len, features = queries.shape
    head_count = features // HEAD
    flat_rows = grad_out.reshape(-1, grad_out.shape[-1])
    grad_attn = jnp.dot(flat_rows, out_proj, preferred_element_type=jnp.float32).astype(jnp.bfloat16)
    grad_attn = grad_attn.reshape(queries.shape)
    span = min(3, frames)
    grid_f, grid_r, grid_c = jnp.meshgrid(jnp.arange(frames, dtype=jnp.int32), jnp.arange(tile_rows, dtype=jnp.int32), jnp.arange(tile_cols, dtype=jnp.int32), indexing='ij')
    start_f = jnp.clip(grid_f.reshape(-1) - 1, 0, frames - span).astype(jnp.int32)
    start_r = jnp.clip(grid_r.reshape(-1) - 1, 0, tile_rows - 3).astype(jnp.int32)
    start_c = jnp.clip(grid_c.reshape(-1) - 1, 0, tile_cols - 3).astype(jnp.int32)
    tile_count = start_f.shape[0]
    zero_idx = jnp.zeros((), jnp.int32)
    softmax_scale = HEAD ** -0.5

    def split_heads(array):
        return jnp.moveaxis(array.reshape(frames, tile_rows, tile_cols, tile_len, head_count, HEAD), 4, 0)

    def join_heads(array):
        return jnp.moveaxis(array, 0, 4).reshape(frames, tile_rows, tile_cols, tile_len, features)

    def one_head(operands):
        query_h, key_h, value_h, grad_h = operands
        both = jnp.stack([key_h, value_h])

        def take(first, second, third):
            return lax.dynamic_slice(both, (zero_idx, first, second, third, zero_idx, zero_idx), (2, span, 3, 3, tile_len, HEAD))

        window = jax.vmap(take)(start_f, start_r, start_c)
        key_blk = window[:, 0].reshape(tile_count, -1, HEAD)
        value_blk = window[:, 1].reshape(tile_count, -1, HEAD)
        query_blk = query_h.reshape(tile_count, tile_len, HEAD)
        grad_blk = grad_h.reshape(tile_count, tile_len, HEAD)
        grad_query, grad_key, grad_value = tile_backward(query_blk, key_blk, value_blk, grad_blk, softmax_scale)
        pieces = jnp.stack([grad_key, grad_value], 1).reshape(tile_count, 2, span, 3, 3, tile_len, HEAD)
        totals = jnp.zeros((2, frames, tile_rows, tile_cols, tile_len, HEAD), jnp.float32)

        def add_one(index, totals):
            start = (zero_idx, start_f[index], start_r[index], start_c[index], zero_idx, zero_idx)
            current = lax.dynamic_slice(totals, start, (2, span, 3, 3, tile_len, HEAD))
            return lax.dynamic_update_slice(totals, current + pieces[index], start)

        totals = lax.fori_loop(0, tile_count, add_one, totals)
        grad_query = grad_query.reshape(frames, tile_rows, tile_cols, tile_len, HEAD).astype(jnp.bfloat16)
        return grad_query, totals[0].astype(jnp.bfloat16), totals[1].astype(jnp.bfloat16)

    grad_q, grad_k, grad_v = lax.map(one_head, (split_heads(queries), split_heads(keys), split_heads(values), split_heads(grad_attn)))
    return (join_heads(grad_q), join_heads(grad_k), join_heads(grad_v))
```

```python
import jax
import jax.numpy as jnp
from jax import lax
from jax.sharding import PartitionSpec as P

HEAD = 128


def doubling_gather(block, steps):
    sizes = {"ha": lax.axis_size("ha"), "wa": lax.axis_size("wa")}
    index = {"ha": lax.axis_index("ha"), "wa": lax.axis_index("wa")}
    buf = block
    for axis, bit in steps:
        count = sizes[axis]
        other = lax.ppermute(buf, axis, [(i, i ^ bit) for i in range(count)])
        low = (index[axis] // bit) % 2 == 0
        buf = jnp.where(low, jnp.concatenate([buf, other], 0), jnp.concatenate([other, buf], 0))
    return buf


def gather_rows(out_proj):
    ha, wa = lax.axis_size("ha"), lax.axis_size("wa")
    ha_bits = [1 << b for b in range(ha.bit_length() - 1)]
    wa_bits = [1 << b for b in range(wa.bit_length() - 1)]
    steps = [("wa", b) for b in reversed(wa_bits)] + [("ha", b) for b in reversed(ha_bits)]
    buf = doubling_gather(out_proj, steps)
    rows, cols = out_proj.shape
    order = list(reversed(steps))
    buf = buf.reshape([2] * len(steps) + [rows, cols])
    natural = [("ha", b) for b in reversed(ha_bits)] + [("wa", b) for b in reversed(wa_bits)]
    perm = [order.index(s) for s in natural] + [len(steps), len(steps) + 1]
    return buf.transpose(perm).reshape(-1, cols)


def pick(length, d):
    if d < 0:
        return slice(length - 1, length)
    if d > 0:
        return slice(0, 1)
    return slice(0, length)


def neighbour_pairs(d_r, d_c):
    ha, wa = lax.axis_size("ha"), lax.axis_size("wa")
    pairs = []
    for i in range(ha):
        for j in range(wa):
            ti, tj = i - d_r, j - d_c
            if 0 <= ti < ha and 0 <= tj < wa:
                pairs.append((i * wa + j, ti * wa + tj))
    return pairs


DIRS = [(-1, -1), (-1, 0), (-1, 1), (0, -1), (0, 1), (1, -1), (1, 0), (1, 1)]


def extended(stacked):
    _, _, rows, cols = stacked.shape[:4]
    out = jnp.pad(stacked, ((0, 0), (0, 0), (1, 1), (1, 1), (0, 0), (0, 0)))
    for d_r, d_c in DIRS:
        piece = stacked[:, :, pick(rows, d_r), pick(cols, d_c)]
        got = lax.ppermute(piece, ("ha", "wa"), neighbour_pairs(d_r, d_c))
        r0 = 0 if d_r < 0 else (rows + 1 if d_r > 0 else 1)
        c0 = 0 if d_c < 0 else (cols + 1 if d_c > 0 else 1)
        out = lax.dynamic_update_slice(out, got, (0, 0, r0, c0, 0, 0))
    return out


def folded(totals):
    rows, cols = totals.shape[2] - 2, totals.shape[3] - 2
    own = totals[:, :, 1:-1, 1:-1]
    for d_r, d_c in DIRS:
        r0 = 0 if d_r < 0 else (rows + 1 if d_r > 0 else 1)
        c0 = 0 if d_c < 0 else (cols + 1 if d_c > 0 else 1)
        nr = rows if d_r == 0 else 1
        nc = cols if d_c == 0 else 1
        piece = totals[:, :, r0 : r0 + nr, c0 : c0 + nc].astype(jnp.bfloat16)
        got = lax.ppermute(piece, ("ha", "wa"), neighbour_pairs(-d_r, -d_c)).astype(jnp.float32)
        rs, cs = pick(rows, d_r), pick(cols, d_c)
        own = own.at[:, :, rs, cs].add(got)
    return own


def local(queries, keys, values, grad_out, out_proj):
    frames, tile_rows, tile_cols, tile_len, columns = queries.shape
    heads = columns // HEAD
    f32, bf16 = jnp.float32, jnp.bfloat16
    whole = lax.all_gather(grad_out, "tp", axis=4, tiled=True)
    weight = gather_rows(out_proj)
    ext = extended(jnp.stack([keys, values]))
    ext_r, ext_c = tile_rows + 2, tile_cols + 2
    row_base = lax.axis_index("ha") * tile_rows
    col_base = lax.axis_index("wa") * tile_cols
    rows_all = tile_rows * lax.axis_size("ha")
    cols_all = tile_cols * lax.axis_size("wa")
    qr = jnp.arange(tile_rows, dtype=jnp.int32)
    qc = jnp.arange(tile_cols, dtype=jnp.int32)
    sr = jnp.clip(row_base + qr - 1, 0, rows_all - 3) - row_base + 1
    sc = jnp.clip(col_base + qc - 1, 0, cols_all - 3) - col_base + 1
    kr = jnp.arange(ext_r, dtype=jnp.int32)
    kc = jnp.arange(ext_c, dtype=jnp.int32)
    in_r = (kr[None, :] >= sr[:, None]) & (kr[None, :] < sr[:, None] + 3)
    in_c = (kc[None, :] >= sc[:, None]) & (kc[None, :] < sc[:, None] + 3)
    inside = in_r[:, None, :, None] & in_c[None, :, None, :]
    inside = inside.reshape(tile_rows * tile_cols, 1, ext_r * ext_c, 1)
    inside = jnp.broadcast_to(inside, (tile_rows * tile_cols, 1, ext_r * ext_c, tile_len))
    inside = inside.reshape(tile_rows * tile_cols, 1, 1, ext_r * ext_c * tile_len)
    q_tiles = tile_rows * tile_cols
    keys_n = ext_r * ext_c * tile_len
    scale = HEAD ** (-0.5)

    key_e = ext[0].reshape(keys_n, heads, HEAD)
    val_e = ext[1].reshape(keys_n, heads, HEAD)
    query = queries.reshape(q_tiles, tile_len, heads, HEAD)

    scores = jnp.einsum("qthd,lhd->qhtl", query, key_e, preferred_element_type=f32) * scale
    scores = jnp.where(inside, scores, -jnp.inf)
    scores = scores - jnp.max(scores, axis=-1, keepdims=True)
    expo = jnp.exp(scores)
    probs = expo / jnp.sum(expo, axis=-1, keepdims=True)
    probs_lo = probs.astype(bf16)

    grad_attn = jnp.dot(
        whole.reshape(-1, whole.shape[-1]), weight, preferred_element_type=f32
    ).astype(bf16)
    grad = grad_attn.reshape(q_tiles, tile_len, heads, HEAD)

    attn = jnp.einsum("qhtl,lhd->qthd", probs_lo, val_e, preferred_element_type=f32)
    delta = jnp.sum(grad.astype(f32) * attn, axis=-1)
    delta = jnp.transpose(delta, (0, 2, 1))[..., None]
    grad_probs = jnp.einsum("qthd,lhd->qhtl", grad, val_e, preferred_element_type=f32)
    grad_scores = (probs * (grad_probs - delta) * scale).astype(bf16)
    grad_q = jnp.einsum("qhtl,lhd->qthd", grad_scores, key_e, preferred_element_type=f32)
    grad_k = jnp.einsum("qhtl,qthd->lhd", grad_scores, query, preferred_element_type=f32)
    grad_v = jnp.einsum("qhtl,qthd->lhd", probs_lo, grad, preferred_element_type=f32)

    grad_queries = grad_q.reshape(queries.shape).astype(bf16)
    totals = jnp.stack([grad_k, grad_v]).reshape(2, frames, ext_r, ext_c, tile_len, columns)
    own = folded(totals)
    return (grad_queries, own[0].astype(bf16), own[1].astype(bf16))


def solution(mesh):
    in_specs = (
        P(None, "ha", "wa", None, "tp"),
        P(None, "ha", "wa", None, "tp"),
        P(None, "ha", "wa", None, "tp"),
        P(None, "ha", "wa", None, "tp"),
        P(("ha", "wa"), "tp"),
    )
    out_specs = (
        P(None, "ha", "wa", None, "tp"),
        P(None, "ha", "wa", None, "tp"),
        P(None, "ha", "wa", None, "tp"),
    )
    return jax.shard_map(local, mesh=mesh, in_specs=in_specs, out_specs=out_specs, check_vma=False)
```

```python
import jax
import jax.numpy as jnp
from jax import lax
from jax.sharding import PartitionSpec as P

HEAD = 128


def doubling_gather(block, steps):
    sizes = {"ha": lax.axis_size("ha"), "wa": lax.axis_size("wa")}
    index = {"ha": lax.axis_index("ha"), "wa": lax.axis_index("wa")}
    buf = block
    for axis, bit in steps:
        count = sizes[axis]
        other = lax.ppermute(buf, axis, [(i, i ^ bit) for i in range(count)])
        low = (index[axis] // bit) % 2 == 0
        buf = jnp.where(low, jnp.concatenate([buf, other], 0), jnp.concatenate([other, buf], 0))
    return buf


def gather_rows(out_proj):
    ha, wa = lax.axis_size("ha"), lax.axis_size("wa")
    ha_bits = [1 << b for b in range(ha.bit_length() - 1)]
    wa_bits = [1 << b for b in range(wa.bit_length() - 1)]
    steps = [("wa", b) for b in reversed(wa_bits)] + [("ha", b) for b in reversed(ha_bits)]
    buf = doubling_gather(out_proj, steps)
    rows, cols = out_proj.shape
    order = list(reversed(steps))
    buf = buf.reshape([2] * len(steps) + [rows, cols])
    natural = [("ha", b) for b in reversed(ha_bits)] + [("wa", b) for b in reversed(wa_bits)]
    perm = [order.index(s) for s in natural] + [len(steps), len(steps) + 1]
    return buf.transpose(perm).reshape(-1, cols)


def pick(length, d):
    if d < 0:
        return slice(length - 1, length)
    if d > 0:
        return slice(0, 1)
    return slice(0, length)


def neighbour_pairs(d_r, d_c):
    ha, wa = lax.axis_size("ha"), lax.axis_size("wa")
    pairs = []
    for i in range(ha):
        for j in range(wa):
            ti, tj = i - d_r, j - d_c
            if 0 <= ti < ha and 0 <= tj < wa:
                pairs.append((i * wa + j, ti * wa + tj))
    return pairs


DIRS = [(-1, -1), (-1, 0), (-1, 1), (0, -1), (0, 1), (1, -1), (1, 0), (1, 1)]


def extended(stacked):
    _, _, rows, cols = stacked.shape[:4]
    out = jnp.pad(stacked, ((0, 0), (0, 0), (1, 1), (1, 1), (0, 0), (0, 0)))
    for d_r, d_c in DIRS:
        piece = stacked[:, :, pick(rows, d_r), pick(cols, d_c)]
        got = lax.ppermute(piece, ("ha", "wa"), neighbour_pairs(d_r, d_c))
        r0 = 0 if d_r < 0 else (rows + 1 if d_r > 0 else 1)
        c0 = 0 if d_c < 0 else (cols + 1 if d_c > 0 else 1)
        out = lax.dynamic_update_slice(out, got, (0, 0, r0, c0, 0, 0))
    return out


def folded(totals):
    rows, cols = totals.shape[2] - 2, totals.shape[3] - 2
    own = totals[:, :, 1:-1, 1:-1]
    for d_r, d_c in DIRS:
        r0 = 0 if d_r < 0 else (rows + 1 if d_r > 0 else 1)
        c0 = 0 if d_c < 0 else (cols + 1 if d_c > 0 else 1)
        nr = rows if d_r == 0 else 1
        nc = cols if d_c == 0 else 1
        piece = totals[:, :, r0 : r0 + nr, c0 : c0 + nc].astype(jnp.bfloat16)
        got = lax.ppermute(piece, ("ha", "wa"), neighbour_pairs(-d_r, -d_c)).astype(jnp.float32)
        rs, cs = pick(rows, d_r), pick(cols, d_c)
        own = own.at[:, :, rs, cs].add(got)
    return own


def local(queries, keys, values, grad_out, out_proj):
    frames, tile_rows, tile_cols, tile_len, columns = queries.shape
    heads = columns // HEAD
    f32, bf16 = jnp.float32, jnp.bfloat16
    whole = lax.all_gather(grad_out, "tp", axis=4, tiled=True)
    weight = lax.all_gather(lax.all_gather(out_proj, "wa", axis=0, tiled=True), "ha", axis=0, tiled=True)
    ext = extended(jnp.stack([keys, values]))
    ext_r, ext_c = tile_rows + 2, tile_cols + 2
    row_base = lax.axis_index("ha") * tile_rows
    col_base = lax.axis_index("wa") * tile_cols
    rows_all = tile_rows * lax.axis_size("ha")
    cols_all = tile_cols * lax.axis_size("wa")
    qr = jnp.arange(tile_rows, dtype=jnp.int32)
    qc = jnp.arange(tile_cols, dtype=jnp.int32)
    sr = jnp.clip(row_base + qr - 1, 0, rows_all - 3) - row_base + 1
    sc = jnp.clip(col_base + qc - 1, 0, cols_all - 3) - col_base + 1
    kr = jnp.arange(ext_r, dtype=jnp.int32)
    kc = jnp.arange(ext_c, dtype=jnp.int32)
    in_r = (kr[None, :] >= sr[:, None]) & (kr[None, :] < sr[:, None] + 3)
    in_c = (kc[None, :] >= sc[:, None]) & (kc[None, :] < sc[:, None] + 3)
    inside = in_r[:, None, :, None] & in_c[None, :, None, :]
    inside = inside.reshape(tile_rows * tile_cols, 1, ext_r * ext_c, 1)
    inside = jnp.broadcast_to(inside, (tile_rows * tile_cols, 1, ext_r * ext_c, tile_len))
    inside = inside.reshape(tile_rows * tile_cols, 1, 1, ext_r * ext_c * tile_len)
    q_tiles = tile_rows * tile_cols
    keys_n = ext_r * ext_c * tile_len
    scale = HEAD ** (-0.5)

    key_e = ext[0].reshape(keys_n, heads, HEAD)
    val_e = ext[1].reshape(keys_n, heads, HEAD)
    query = queries.reshape(q_tiles, tile_len, heads, HEAD)

    scores = jnp.einsum("qthd,lhd->qhtl", query, key_e, preferred_element_type=f32) * scale
    scores = jnp.where(inside, scores, -jnp.inf)
    scores = scores - jnp.max(scores, axis=-1, keepdims=True)
    expo = jnp.exp(scores)
    probs = expo / jnp.sum(expo, axis=-1, keepdims=True)
    probs_lo = probs.astype(bf16)

    grad_attn = jnp.dot(
        whole.reshape(-1, whole.shape[-1]), weight, preferred_element_type=f32
    ).astype(bf16)
    grad = grad_attn.reshape(q_tiles, tile_len, heads, HEAD)

    attn = jnp.einsum("qhtl,lhd->qthd", probs_lo, val_e, preferred_element_type=f32)
    delta = jnp.sum(grad.astype(f32) * attn, axis=-1)
    delta = jnp.transpose(delta, (0, 2, 1))[..., None]
    grad_probs = jnp.einsum("qthd,lhd->qhtl", grad, val_e, preferred_element_type=f32)
    grad_scores = (probs * (grad_probs - delta) * scale).astype(bf16)
    grad_q = jnp.einsum("qhtl,lhd->qthd", grad_scores, key_e, preferred_element_type=f32)
    grad_k = jnp.einsum("qhtl,qthd->lhd", grad_scores, query, preferred_element_type=f32)
    grad_v = jnp.einsum("qhtl,qthd->lhd", probs_lo, grad, preferred_element_type=f32)

    grad_queries = grad_q.reshape(queries.shape).astype(bf16)
    totals = jnp.stack([grad_k, grad_v]).reshape(2, frames, ext_r, ext_c, tile_len, columns)
    own = folded(totals)
    return (grad_queries, own[0].astype(bf16), own[1].astype(bf16))


def solution(mesh):
    in_specs = (
        P(None, "ha", "wa", None, "tp"),
        P(None, "ha", "wa", None, "tp"),
        P(None, "ha", "wa", None, "tp"),
        P(None, "ha", "wa", None, "tp"),
        P(("ha", "wa"), "tp"),
    )
    out_specs = (
        P(None, "ha", "wa", None, "tp"),
        P(None, "ha", "wa", None, "tp"),
        P(None, "ha", "wa", None, "tp"),
    )
    return jax.shard_map(local, mesh=mesh, in_specs=in_specs, out_specs=out_specs, check_vma=False)
```

```python
import jax
import jax.numpy as jnp
from jax import lax
from jax.sharding import PartitionSpec as P

HEAD = 128


def doubling_gather(block, steps):
    sizes = {"ha": lax.axis_size("ha"), "wa": lax.axis_size("wa")}
    index = {"ha": lax.axis_index("ha"), "wa": lax.axis_index("wa")}
    buf = block
    for axis, bit in steps:
        count = sizes[axis]
        other = lax.ppermute(buf, axis, [(i, i ^ bit) for i in range(count)])
        low = (index[axis] // bit) % 2 == 0
        buf = jnp.where(low, jnp.concatenate([buf, other], 0), jnp.concatenate([other, buf], 0))
    return buf


def gather_rows(out_proj):
    ha, wa = lax.axis_size("ha"), lax.axis_size("wa")
    ha_bits = [1 << b for b in range(ha.bit_length() - 1)]
    wa_bits = [1 << b for b in range(wa.bit_length() - 1)]
    steps = [("wa", b) for b in reversed(wa_bits)] + [("ha", b) for b in reversed(ha_bits)]
    buf = doubling_gather(out_proj, steps)
    rows, cols = out_proj.shape
    order = list(reversed(steps))
    buf = buf.reshape([2] * len(steps) + [rows, cols])
    natural = [("ha", b) for b in reversed(ha_bits)] + [("wa", b) for b in reversed(wa_bits)]
    perm = [order.index(s) for s in natural] + [len(steps), len(steps) + 1]
    return buf.transpose(perm).reshape(-1, cols)


def shift_gather(block, axis):
    count, index = lax.axis_size(axis), lax.axis_index(axis)
    rows = block.shape[0]
    buf = jnp.zeros((count * rows,) + block.shape[1:], block.dtype)
    buf = lax.dynamic_update_slice(buf, block, (index * rows, 0))
    for shift in range(1, count):
        got = lax.ppermute(block, axis, [(k, (k + shift) % count) for k in range(count)])
        buf = lax.dynamic_update_slice(buf, got, (((index - shift) % count) * rows, 0))
    return buf


def pick(length, d):
    if d < 0:
        return slice(length - 1, length)
    if d > 0:
        return slice(0, 1)
    return slice(0, length)


def neighbour_pairs(d_r, d_c):
    ha, wa = lax.axis_size("ha"), lax.axis_size("wa")
    pairs = []
    for i in range(ha):
        for j in range(wa):
            ti, tj = i - d_r, j - d_c
            if 0 <= ti < ha and 0 <= tj < wa:
                pairs.append((i * wa + j, ti * wa + tj))
    return pairs


DIRS = [(-1, -1), (-1, 0), (-1, 1), (0, -1), (0, 1), (1, -1), (1, 0), (1, 1)]


def extended(stacked):
    _, _, rows, cols = stacked.shape[:4]
    out = jnp.pad(stacked, ((0, 0), (0, 0), (1, 1), (1, 1), (0, 0), (0, 0)))
    for d_r, d_c in DIRS:
        piece = stacked[:, :, pick(rows, d_r), pick(cols, d_c)]
        got = lax.ppermute(piece, ("ha", "wa"), neighbour_pairs(d_r, d_c))
        r0 = 0 if d_r < 0 else (rows + 1 if d_r > 0 else 1)
        c0 = 0 if d_c < 0 else (cols + 1 if d_c > 0 else 1)
        out = lax.dynamic_update_slice(out, got, (0, 0, r0, c0, 0, 0))
    return out


def folded(totals):
    rows, cols = totals.shape[2] - 2, totals.shape[3] - 2
    own = totals[:, :, 1:-1, 1:-1]
    for d_r, d_c in DIRS:
        r0 = 0 if d_r < 0 else (rows + 1 if d_r > 0 else 1)
        c0 = 0 if d_c < 0 else (cols + 1 if d_c > 0 else 1)
        nr = rows if d_r == 0 else 1
        nc = cols if d_c == 0 else 1
        piece = totals[:, :, r0 : r0 + nr, c0 : c0 + nc].astype(jnp.bfloat16)
        got = lax.ppermute(piece, ("ha", "wa"), neighbour_pairs(-d_r, -d_c)).astype(jnp.float32)
        rs, cs = pick(rows, d_r), pick(cols, d_c)
        own = own.at[:, :, rs, cs].add(got)
    return own


def local(queries, keys, values, grad_out, out_proj):
    frames, tile_rows, tile_cols, tile_len, columns = queries.shape
    heads = columns // HEAD
    f32, bf16 = jnp.float32, jnp.bfloat16
    whole = lax.all_gather(grad_out, "tp", axis=4, tiled=True)
    weight = shift_gather(shift_gather(out_proj, "wa"), "ha")
    ext = extended(jnp.stack([keys, values]))
    ext_r, ext_c = tile_rows + 2, tile_cols + 2
    row_base = lax.axis_index("ha") * tile_rows
    col_base = lax.axis_index("wa") * tile_cols
    rows_all = tile_rows * lax.axis_size("ha")
    cols_all = tile_cols * lax.axis_size("wa")
    qr = jnp.arange(tile_rows, dtype=jnp.int32)
    qc = jnp.arange(tile_cols, dtype=jnp.int32)
    sr = jnp.clip(row_base + qr - 1, 0, rows_all - 3) - row_base + 1
    sc = jnp.clip(col_base + qc - 1, 0, cols_all - 3) - col_base + 1
    kr = jnp.arange(ext_r, dtype=jnp.int32)
    kc = jnp.arange(ext_c, dtype=jnp.int32)
    in_r = (kr[None, :] >= sr[:, None]) & (kr[None, :] < sr[:, None] + 3)
    in_c = (kc[None, :] >= sc[:, None]) & (kc[None, :] < sc[:, None] + 3)
    inside = in_r[:, None, :, None] & in_c[None, :, None, :]
    inside = inside.reshape(tile_rows * tile_cols, 1, ext_r * ext_c, 1)
    inside = jnp.broadcast_to(inside, (tile_rows * tile_cols, 1, ext_r * ext_c, tile_len))
    inside = inside.reshape(tile_rows * tile_cols, 1, 1, ext_r * ext_c * tile_len)
    q_tiles = tile_rows * tile_cols
    keys_n = ext_r * ext_c * tile_len
    scale = HEAD ** (-0.5)

    key_e = ext[0].reshape(keys_n, heads, HEAD)
    val_e = ext[1].reshape(keys_n, heads, HEAD)
    query = queries.reshape(q_tiles, tile_len, heads, HEAD)

    scores = jnp.einsum("qthd,lhd->qhtl", query, key_e, preferred_element_type=f32) * scale
    scores = jnp.where(inside, scores, -jnp.inf)
    scores = scores - jnp.max(scores, axis=-1, keepdims=True)
    expo = jnp.exp(scores)
    probs = expo / jnp.sum(expo, axis=-1, keepdims=True)
    probs_lo = probs.astype(bf16)

    grad_attn = jnp.dot(
        whole.reshape(-1, whole.shape[-1]), weight, preferred_element_type=f32
    ).astype(bf16)
    grad = grad_attn.reshape(q_tiles, tile_len, heads, HEAD)

    attn = jnp.einsum("qhtl,lhd->qthd", probs_lo, val_e, preferred_element_type=f32)
    delta = jnp.sum(grad.astype(f32) * attn, axis=-1)
    delta = jnp.transpose(delta, (0, 2, 1))[..., None]
    grad_probs = jnp.einsum("qthd,lhd->qhtl", grad, val_e, preferred_element_type=f32)
    grad_scores = (probs * (grad_probs - delta) * scale).astype(bf16)
    grad_q = jnp.einsum("qhtl,lhd->qthd", grad_scores, key_e, preferred_element_type=f32)
    grad_k = jnp.einsum("qhtl,qthd->lhd", grad_scores, query, preferred_element_type=f32)
    grad_v = jnp.einsum("qhtl,qthd->lhd", probs_lo, grad, preferred_element_type=f32)

    grad_queries = grad_q.reshape(queries.shape).astype(bf16)
    totals = jnp.stack([grad_k, grad_v]).reshape(2, frames, ext_r, ext_c, tile_len, columns)
    own = folded(totals)
    return (grad_queries, own[0].astype(bf16), own[1].astype(bf16))


def solution(mesh):
    in_specs = (
        P(None, "ha", "wa", None, "tp"),
        P(None, "ha", "wa", None, "tp"),
        P(None, "ha", "wa", None, "tp"),
        P(None, "ha", "wa", None, "tp"),
        P(("ha", "wa"), "tp"),
    )
    out_specs = (
        P(None, "ha", "wa", None, "tp"),
        P(None, "ha", "wa", None, "tp"),
        P(None, "ha", "wa", None, "tp"),
    )
    return jax.shard_map(local, mesh=mesh, in_specs=in_specs, out_specs=out_specs, check_vma=False)
```

```python
import jax
import jax.numpy as jnp
from jax import lax
from jax.sharding import PartitionSpec as P

HEAD = 128


def doubling_gather(block, steps):
    sizes = {"ha": lax.axis_size("ha"), "wa": lax.axis_size("wa")}
    index = {"ha": lax.axis_index("ha"), "wa": lax.axis_index("wa")}
    buf = block
    for axis, bit in steps:
        count = sizes[axis]
        other = lax.ppermute(buf, axis, [(i, i ^ bit) for i in range(count)])
        low = (index[axis] // bit) % 2 == 0
        buf = jnp.where(low, jnp.concatenate([buf, other], 0), jnp.concatenate([other, buf], 0))
    return buf


def gather_rows(out_proj):
    ha, wa = lax.axis_size("ha"), lax.axis_size("wa")
    ha_bits = [1 << b for b in range(ha.bit_length() - 1)]
    wa_bits = [1 << b for b in range(wa.bit_length() - 1)]
    steps = [("wa", b) for b in reversed(wa_bits)] + [("ha", b) for b in reversed(ha_bits)]
    buf = doubling_gather(out_proj, steps)
    rows, cols = out_proj.shape
    order = list(reversed(steps))
    buf = buf.reshape([2] * len(steps) + [rows, cols])
    natural = [("ha", b) for b in reversed(ha_bits)] + [("wa", b) for b in reversed(wa_bits)]
    perm = [order.index(s) for s in natural] + [len(steps), len(steps) + 1]
    return buf.transpose(perm).reshape(-1, cols)


def passed_along(value, axis, steps):
    count = lax.axis_size(axis)
    first, last = (max(0, -steps), min(count, count - steps))
    return lax.ppermute(value, axis, [(source, source + steps) for source in range(first, last)])


def extended_2(array, sides, width):
    for axis, dim in sides:
        peers, length = (lax.axis_size(axis), array.shape[dim])
        up = [(i, (i + 1) % peers) for i in range(peers - 1)]
        down = [(j, i) for i, j in up]
        last = lax.slice_in_dim(array, length - width, length, axis=dim)
        first = lax.slice_in_dim(array, 0, width, axis=dim)
        before = lax.ppermute(last, axis, up)
        after = lax.ppermute(first, axis, down)
        array = jnp.concatenate([before, array, after], axis=dim)
    return array


def fold_cols(totals):
    from_left = passed_along(totals[:, :, :, -1].astype(jnp.bfloat16), "wa", 1).astype(jnp.float32)
    from_right = passed_along(totals[:, :, :, 0].astype(jnp.bfloat16), "wa", -1).astype(jnp.float32)
    inner = totals[:, :, :, 1:-1]
    inner = inner.at[:, :, :, 0].add(from_left)
    return inner.at[:, :, :, -1].add(from_right)


def fold_rows(totals):
    from_above = passed_along(totals[:, :, -1].astype(jnp.bfloat16), "ha", 1).astype(jnp.float32)
    from_below = passed_along(totals[:, :, 0].astype(jnp.bfloat16), "ha", -1).astype(jnp.float32)
    inner = totals[:, :, 1:-1]
    inner = inner.at[:, :, 0].add(from_above)
    return inner.at[:, :, -1].add(from_below)


def pick(length, d):
    if d < 0:
        return slice(length - 1, length)
    if d > 0:
        return slice(0, 1)
    return slice(0, length)


def neighbour_pairs(d_r, d_c):
    ha, wa = lax.axis_size("ha"), lax.axis_size("wa")
    pairs = []
    for i in range(ha):
        for j in range(wa):
            ti, tj = i - d_r, j - d_c
            if 0 <= ti < ha and 0 <= tj < wa:
                pairs.append((i * wa + j, ti * wa + tj))
    return pairs


DIRS = [(-1, -1), (-1, 0), (-1, 1), (0, -1), (0, 1), (1, -1), (1, 0), (1, 1)]


def extended(stacked):
    _, _, rows, cols = stacked.shape[:4]
    out = jnp.pad(stacked, ((0, 0), (0, 0), (1, 1), (1, 1), (0, 0), (0, 0)))
    for d_r, d_c in DIRS:
        piece = stacked[:, :, pick(rows, d_r), pick(cols, d_c)]
        got = lax.ppermute(piece, ("ha", "wa"), neighbour_pairs(d_r, d_c))
        r0 = 0 if d_r < 0 else (rows + 1 if d_r > 0 else 1)
        c0 = 0 if d_c < 0 else (cols + 1 if d_c > 0 else 1)
        out = lax.dynamic_update_slice(out, got, (0, 0, r0, c0, 0, 0))
    return out


def folded(totals):
    rows, cols = totals.shape[2] - 2, totals.shape[3] - 2
    own = totals[:, :, 1:-1, 1:-1]
    for d_r, d_c in DIRS:
        r0 = 0 if d_r < 0 else (rows + 1 if d_r > 0 else 1)
        c0 = 0 if d_c < 0 else (cols + 1 if d_c > 0 else 1)
        nr = rows if d_r == 0 else 1
        nc = cols if d_c == 0 else 1
        piece = totals[:, :, r0 : r0 + nr, c0 : c0 + nc].astype(jnp.bfloat16)
        got = lax.ppermute(piece, ("ha", "wa"), neighbour_pairs(-d_r, -d_c)).astype(jnp.float32)
        rs, cs = pick(rows, d_r), pick(cols, d_c)
        own = own.at[:, :, rs, cs].add(got)
    return own


def local(queries, keys, values, grad_out, out_proj):
    frames, tile_rows, tile_cols, tile_len, columns = queries.shape
    heads = columns // HEAD
    f32, bf16 = jnp.float32, jnp.bfloat16
    whole = lax.all_gather(grad_out, "tp", axis=4, tiled=True)
    weight = gather_rows(out_proj)
    ext = extended_2(jnp.stack([keys, values]), (("ha", 2), ("wa", 3)), 1)
    ext_r, ext_c = tile_rows + 2, tile_cols + 2
    row_base = lax.axis_index("ha") * tile_rows
    col_base = lax.axis_index("wa") * tile_cols
    rows_all = tile_rows * lax.axis_size("ha")
    cols_all = tile_cols * lax.axis_size("wa")
    qr = jnp.arange(tile_rows, dtype=jnp.int32)
    qc = jnp.arange(tile_cols, dtype=jnp.int32)
    sr = jnp.clip(row_base + qr - 1, 0, rows_all - 3) - row_base + 1
    sc = jnp.clip(col_base + qc - 1, 0, cols_all - 3) - col_base + 1
    kr = jnp.arange(ext_r, dtype=jnp.int32)
    kc = jnp.arange(ext_c, dtype=jnp.int32)
    in_r = (kr[None, :] >= sr[:, None]) & (kr[None, :] < sr[:, None] + 3)
    in_c = (kc[None, :] >= sc[:, None]) & (kc[None, :] < sc[:, None] + 3)
    inside = in_r[:, None, :, None] & in_c[None, :, None, :]
    inside = inside.reshape(tile_rows * tile_cols, 1, ext_r * ext_c, 1)
    inside = jnp.broadcast_to(inside, (tile_rows * tile_cols, 1, ext_r * ext_c, tile_len))
    inside = inside.reshape(tile_rows * tile_cols, 1, 1, ext_r * ext_c * tile_len)
    q_tiles = tile_rows * tile_cols
    keys_n = ext_r * ext_c * tile_len
    scale = HEAD ** (-0.5)

    key_e = ext[0].reshape(keys_n, heads, HEAD)
    val_e = ext[1].reshape(keys_n, heads, HEAD)
    query = queries.reshape(q_tiles, tile_len, heads, HEAD)

    scores = jnp.einsum("qthd,lhd->qhtl", query, key_e, preferred_element_type=f32) * scale
    scores = jnp.where(inside, scores, -jnp.inf)
    scores = scores - jnp.max(scores, axis=-1, keepdims=True)
    expo = jnp.exp(scores)
    probs = expo / jnp.sum(expo, axis=-1, keepdims=True)
    probs_lo = probs.astype(bf16)

    grad_attn = jnp.dot(
        whole.reshape(-1, whole.shape[-1]), weight, preferred_element_type=f32
    ).astype(bf16)
    grad = grad_attn.reshape(q_tiles, tile_len, heads, HEAD)

    attn = jnp.einsum("qhtl,lhd->qthd", probs_lo, val_e, preferred_element_type=f32)
    delta = jnp.sum(grad.astype(f32) * attn, axis=-1)
    delta = jnp.transpose(delta, (0, 2, 1))[..., None]
    grad_probs = jnp.einsum("qthd,lhd->qhtl", grad, val_e, preferred_element_type=f32)
    grad_scores = (probs * (grad_probs - delta) * scale).astype(bf16)
    grad_q = jnp.einsum("qhtl,lhd->qthd", grad_scores, key_e, preferred_element_type=f32)
    grad_k = jnp.einsum("qhtl,qthd->lhd", grad_scores, query, preferred_element_type=f32)
    grad_v = jnp.einsum("qhtl,qthd->lhd", probs_lo, grad, preferred_element_type=f32)

    grad_queries = grad_q.reshape(queries.shape).astype(bf16)
    totals = jnp.stack([grad_k, grad_v]).reshape(2, frames, ext_r, ext_c, tile_len, columns)
    own = fold_rows(fold_cols(totals))
    return (grad_queries, own[0].astype(bf16), own[1].astype(bf16))


def solution(mesh):
    in_specs = (
        P(None, "ha", "wa", None, "tp"),
        P(None, "ha", "wa", None, "tp"),
        P(None, "ha", "wa", None, "tp"),
        P(None, "ha", "wa", None, "tp"),
        P(("ha", "wa"), "tp"),
    )
    out_specs = (
        P(None, "ha", "wa", None, "tp"),
        P(None, "ha", "wa", None, "tp"),
        P(None, "ha", "wa", None, "tp"),
    )
    return jax.shard_map(local, mesh=mesh, in_specs=in_specs, out_specs=out_specs, check_vma=False)
```

```python
import jax
import jax.numpy as jnp
from jax import lax
from jax.sharding import PartitionSpec as P

HEAD = 128


def doubling_gather(block, steps):
    sizes = {"ha": lax.axis_size("ha"), "wa": lax.axis_size("wa")}
    index = {"ha": lax.axis_index("ha"), "wa": lax.axis_index("wa")}
    buf = block
    for axis, bit in steps:
        count = sizes[axis]
        other = lax.ppermute(buf, axis, [(i, i ^ bit) for i in range(count)])
        low = (index[axis] // bit) % 2 == 0
        buf = jnp.where(low, jnp.concatenate([buf, other], 0), jnp.concatenate([other, buf], 0))
    return buf


def gather_rows(out_proj):
    ha, wa = lax.axis_size("ha"), lax.axis_size("wa")
    ha_bits = [1 << b for b in range(ha.bit_length() - 1)]
    wa_bits = [1 << b for b in range(wa.bit_length() - 1)]
    steps = [("wa", b) for b in reversed(wa_bits)] + [("ha", b) for b in reversed(ha_bits)]
    buf = doubling_gather(out_proj, steps)
    rows, cols = out_proj.shape
    order = list(reversed(steps))
    buf = buf.reshape([2] * len(steps) + [rows, cols])
    natural = [("ha", b) for b in reversed(ha_bits)] + [("wa", b) for b in reversed(wa_bits)]
    perm = [order.index(s) for s in natural] + [len(steps), len(steps) + 1]
    return buf.transpose(perm).reshape(-1, cols)


def pick(length, d):
    if d < 0:
        return slice(length - 1, length)
    if d > 0:
        return slice(0, 1)
    return slice(0, length)


def neighbour_pairs(d_r, d_c):
    ha, wa = lax.axis_size("ha"), lax.axis_size("wa")
    pairs = []
    for i in range(ha):
        for j in range(wa):
            ti, tj = i - d_r, j - d_c
            if 0 <= ti < ha and 0 <= tj < wa:
                pairs.append((i * wa + j, ti * wa + tj))
    return pairs


DIRS = [(-1, -1), (-1, 0), (-1, 1), (0, -1), (0, 1), (1, -1), (1, 0), (1, 1)]


def extended(stacked):
    _, _, rows, cols = stacked.shape[:4]
    out = jnp.pad(stacked, ((0, 0), (0, 0), (1, 1), (1, 1), (0, 0), (0, 0)))
    for d_r, d_c in DIRS:
        piece = stacked[:, :, pick(rows, d_r), pick(cols, d_c)]
        got = lax.ppermute(piece, ("ha", "wa"), neighbour_pairs(d_r, d_c))
        r0 = 0 if d_r < 0 else (rows + 1 if d_r > 0 else 1)
        c0 = 0 if d_c < 0 else (cols + 1 if d_c > 0 else 1)
        out = lax.dynamic_update_slice(out, got, (0, 0, r0, c0, 0, 0))
    return out


def folded(grad_k, grad_v):
    rows, cols = grad_k.shape[1] - 2, grad_k.shape[2] - 2
    own_k = grad_k[:, 1:-1, 1:-1]
    own_v = grad_v[:, 1:-1, 1:-1]
    for d_r, d_c in DIRS:
        r0 = 0 if d_r < 0 else (rows + 1 if d_r > 0 else 1)
        c0 = 0 if d_c < 0 else (cols + 1 if d_c > 0 else 1)
        nr = rows if d_r == 0 else 1
        nc = cols if d_c == 0 else 1
        piece = jnp.stack(
            [grad_k[:, r0 : r0 + nr, c0 : c0 + nc], grad_v[:, r0 : r0 + nr, c0 : c0 + nc]]
        ).astype(jnp.bfloat16)
        got = lax.ppermute(piece, ("ha", "wa"), neighbour_pairs(-d_r, -d_c)).astype(jnp.float32)
        rs, cs = pick(rows, d_r), pick(cols, d_c)
        own_k = own_k.at[:, rs, cs].add(got[0])
        own_v = own_v.at[:, rs, cs].add(got[1])
    return own_k, own_v


def local(queries, keys, values, grad_out, out_proj):
    frames, tile_rows, tile_cols, tile_len, columns = queries.shape
    heads = columns // HEAD
    f32, bf16 = jnp.float32, jnp.bfloat16
    whole = lax.all_gather(grad_out, "tp", axis=4, tiled=True)
    weight = gather_rows(out_proj)

    def head_major(array):
        split = array.reshape(frames * tile_rows, tile_cols, tile_len, heads, HEAD)
        return jnp.transpose(split, (3, 0, 1, 2, 4))

    def head_minor(array):
        return jnp.transpose(array, (1, 2, 3, 0, 4)).reshape(queries.shape)

    ext = extended(jnp.stack([head_major(keys), head_major(values)]))
    ext_r, ext_c = tile_rows + 2, tile_cols + 2
    row_base = lax.axis_index("ha") * tile_rows
    col_base = lax.axis_index("wa") * tile_cols
    rows_all = tile_rows * lax.axis_size("ha")
    cols_all = tile_cols * lax.axis_size("wa")
    qr = jnp.arange(tile_rows, dtype=jnp.int32)
    qc = jnp.arange(tile_cols, dtype=jnp.int32)
    sr = jnp.clip(row_base + qr - 1, 0, rows_all - 3) - row_base + 1
    sc = jnp.clip(col_base + qc - 1, 0, cols_all - 3) - col_base + 1
    kr = jnp.arange(ext_r, dtype=jnp.int32)
    kc = jnp.arange(ext_c, dtype=jnp.int32)
    in_r = (kr[None, :] >= sr[:, None]) & (kr[None, :] < sr[:, None] + 3)
    in_c = (kc[None, :] >= sc[:, None]) & (kc[None, :] < sc[:, None] + 3)
    inside = in_r[:, None, :, None] & in_c[None, :, None, :]
    inside = inside.reshape(tile_rows * tile_cols, 1, ext_r * ext_c, 1)
    inside = jnp.broadcast_to(inside, (tile_rows * tile_cols, 1, ext_r * ext_c, tile_len))
    inside = inside.reshape(1, tile_rows * tile_cols, 1, ext_r * ext_c * tile_len)
    q_tiles = tile_rows * tile_cols
    keys_n = ext_r * ext_c * tile_len
    scale = HEAD ** (-0.5)

    key_e = ext[0].reshape(heads, keys_n, HEAD)
    val_e = ext[1].reshape(heads, keys_n, HEAD)
    query = head_major(queries).reshape(heads, q_tiles, tile_len, HEAD)

    scores = jnp.einsum("hqtd,hld->hqtl", query, key_e, preferred_element_type=f32) * scale
    scores = jnp.where(inside, scores, -jnp.inf)
    scores = scores - jnp.max(scores, axis=-1, keepdims=True)
    expo = jnp.exp(scores)
    probs = expo / jnp.sum(expo, axis=-1, keepdims=True)
    probs_lo = probs.astype(bf16)

    grad_attn = jnp.dot(
        whole.reshape(-1, whole.shape[-1]), weight, preferred_element_type=f32
    ).astype(bf16)
    grad = head_major(grad_attn.reshape(queries.shape)).reshape(heads, q_tiles, tile_len, HEAD)

    attn = jnp.einsum("hqtl,hld->hqtd", probs_lo, val_e, preferred_element_type=f32)
    delta = jnp.sum(grad.astype(f32) * attn, axis=-1, keepdims=True)
    grad_probs = jnp.einsum("hqtd,hld->hqtl", grad, val_e, preferred_element_type=f32)
    grad_scores = (probs * (grad_probs - delta) * scale).astype(bf16)
    grad_q = jnp.einsum("hqtl,hld->hqtd", grad_scores, key_e, preferred_element_type=f32)
    grad_k = jnp.einsum("hqtl,hqtd->hld", grad_scores, query, preferred_element_type=f32)
    grad_v = jnp.einsum("hqtl,hqtd->hld", probs_lo, grad, preferred_element_type=f32)

    grad_q = grad_q.astype(bf16).reshape(heads, frames * tile_rows, tile_cols, tile_len, HEAD)
    shape_e = (heads, frames * ext_r, ext_c, tile_len, HEAD)
    own_k, own_v = folded(grad_k.reshape(shape_e), grad_v.reshape(shape_e))
    return (head_minor(grad_q), head_minor(own_k.astype(bf16)), head_minor(own_v.astype(bf16)))


def solution(mesh):
    in_specs = (
        P(None, "ha", "wa", None, "tp"),
        P(None, "ha", "wa", None, "tp"),
        P(None, "ha", "wa", None, "tp"),
        P(None, "ha", "wa", None, "tp"),
        P(("ha", "wa"), "tp"),
    )
    out_specs = (
        P(None, "ha", "wa", None, "tp"),
        P(None, "ha", "wa", None, "tp"),
        P(None, "ha", "wa", None, "tp"),
    )
    return jax.shard_map(local, mesh=mesh, in_specs=in_specs, out_specs=out_specs, check_vma=False)
```

```python
import jax
import jax.numpy as jnp
from jax import lax
from jax.sharding import PartitionSpec as P

HEAD = 128


def doubling_gather(block, steps):
    sizes = {"ha": lax.axis_size("ha"), "wa": lax.axis_size("wa")}
    index = {"ha": lax.axis_index("ha"), "wa": lax.axis_index("wa")}
    buf = block
    for axis, bit in steps:
        count = sizes[axis]
        other = lax.ppermute(buf, axis, [(i, i ^ bit) for i in range(count)])
        low = (index[axis] // bit) % 2 == 0
        buf = jnp.where(low, jnp.concatenate([buf, other], 0), jnp.concatenate([other, buf], 0))
    return buf


def gather_rows(out_proj):
    ha, wa = lax.axis_size("ha"), lax.axis_size("wa")
    ha_bits = [1 << b for b in range(ha.bit_length() - 1)]
    wa_bits = [1 << b for b in range(wa.bit_length() - 1)]
    steps = [("wa", b) for b in reversed(wa_bits)] + [("ha", b) for b in reversed(ha_bits)]
    buf = doubling_gather(out_proj, steps)
    rows, cols = out_proj.shape
    order = list(reversed(steps))
    buf = buf.reshape([2] * len(steps) + [rows, cols])
    natural = [("ha", b) for b in reversed(ha_bits)] + [("wa", b) for b in reversed(wa_bits)]
    perm = [order.index(s) for s in natural] + [len(steps), len(steps) + 1]
    return buf.transpose(perm).reshape(-1, cols)


def pick(length, d):
    if d < 0:
        return slice(length - 1, length)
    if d > 0:
        return slice(0, 1)
    return slice(0, length)


def neighbour_pairs(d_r, d_c):
    ha, wa = lax.axis_size("ha"), lax.axis_size("wa")
    pairs = []
    for i in range(ha):
        for j in range(wa):
            ti, tj = i - d_r, j - d_c
            if 0 <= ti < ha and 0 <= tj < wa:
                pairs.append((i * wa + j, ti * wa + tj))
    return pairs


DIRS = [(-1, -1), (-1, 0), (-1, 1), (0, -1), (0, 1), (1, -1), (1, 0), (1, 1)]


def extended(stacked):
    _, _, rows, cols = stacked.shape[:4]
    out = jnp.pad(stacked, ((0, 0), (0, 0), (1, 1), (1, 1), (0, 0), (0, 0)))
    for d_r, d_c in DIRS:
        piece = stacked[:, :, pick(rows, d_r), pick(cols, d_c)]
        got = lax.ppermute(piece, ("ha", "wa"), neighbour_pairs(d_r, d_c))
        r0 = 0 if d_r < 0 else (rows + 1 if d_r > 0 else 1)
        c0 = 0 if d_c < 0 else (cols + 1 if d_c > 0 else 1)
        out = lax.dynamic_update_slice(out, got, (0, 0, r0, c0, 0, 0))
    return out


def folded(grad_k, grad_v):
    rows, cols = grad_k.shape[1] - 2, grad_k.shape[2] - 2
    own_k = grad_k[:, 1:-1, 1:-1]
    own_v = grad_v[:, 1:-1, 1:-1]
    for d_r, d_c in DIRS:
        r0 = 0 if d_r < 0 else (rows + 1 if d_r > 0 else 1)
        c0 = 0 if d_c < 0 else (cols + 1 if d_c > 0 else 1)
        nr = rows if d_r == 0 else 1
        nc = cols if d_c == 0 else 1
        piece = jnp.stack(
            [grad_k[:, r0 : r0 + nr, c0 : c0 + nc], grad_v[:, r0 : r0 + nr, c0 : c0 + nc]]
        ).astype(jnp.bfloat16)
        got = lax.ppermute(piece, ("ha", "wa"), neighbour_pairs(-d_r, -d_c)).astype(jnp.float32)
        rs, cs = pick(rows, d_r), pick(cols, d_c)
        own_k = own_k.at[:, rs, cs].add(got[0])
        own_v = own_v.at[:, rs, cs].add(got[1])
    return own_k, own_v


def local(queries, keys, values, grad_out, out_proj):
    frames, tile_rows, tile_cols, tile_len, columns = queries.shape
    heads = columns // HEAD
    f32, bf16 = jnp.float32, jnp.bfloat16
    whole = lax.all_gather(grad_out, "tp", axis=4, tiled=True)
    group = lax.axis_size("ha") * lax.axis_size("wa")
    copies = jnp.broadcast_to(out_proj[None], (group,) + out_proj.shape).reshape(-1, out_proj.shape[1])
    weight = lax.all_to_all(copies, ("ha", "wa"), 0, 0, tiled=True)

    def head_major(array):
        split = array.reshape(frames * tile_rows, tile_cols, tile_len, heads, HEAD)
        return jnp.transpose(split, (3, 0, 1, 2, 4))

    def head_minor(array):
        return jnp.transpose(array, (1, 2, 3, 0, 4)).reshape(queries.shape)

    ext = extended(jnp.stack([head_major(keys), head_major(values)]))
    ext_r, ext_c = tile_rows + 2, tile_cols + 2
    row_base = lax.axis_index("ha") * tile_rows
    col_base = lax.axis_index("wa") * tile_cols
    rows_all = tile_rows * lax.axis_size("ha")
    cols_all = tile_cols * lax.axis_size("wa")
    qr = jnp.arange(tile_rows, dtype=jnp.int32)
    qc = jnp.arange(tile_cols, dtype=jnp.int32)
    sr = jnp.clip(row_base + qr - 1, 0, rows_all - 3) - row_base + 1
    sc = jnp.clip(col_base + qc - 1, 0, cols_all - 3) - col_base + 1
    kr = jnp.arange(ext_r, dtype=jnp.int32)
    kc = jnp.arange(ext_c, dtype=jnp.int32)
    in_r = (kr[None, :] >= sr[:, None]) & (kr[None, :] < sr[:, None] + 3)
    in_c = (kc[None, :] >= sc[:, None]) & (kc[None, :] < sc[:, None] + 3)
    inside = in_r[:, None, :, None] & in_c[None, :, None, :]
    inside = inside.reshape(tile_rows * tile_cols, 1, ext_r * ext_c, 1)
    inside = jnp.broadcast_to(inside, (tile_rows * tile_cols, 1, ext_r * ext_c, tile_len))
    inside = inside.reshape(1, tile_rows * tile_cols, 1, ext_r * ext_c * tile_len)
    q_tiles = tile_rows * tile_cols
    keys_n = ext_r * ext_c * tile_len
    scale = HEAD ** (-0.5)

    key_e = ext[0].reshape(heads, keys_n, HEAD)
    val_e = ext[1].reshape(heads, keys_n, HEAD)
    query = head_major(queries).reshape(heads, q_tiles, tile_len, HEAD)

    scores = jnp.einsum("hqtd,hld->hqtl", query, key_e, preferred_element_type=f32) * scale
    scores = jnp.where(inside, scores, -jnp.inf)
    scores = scores - jnp.max(scores, axis=-1, keepdims=True)
    expo = jnp.exp(scores)
    probs = expo / jnp.sum(expo, axis=-1, keepdims=True)
    probs_lo = probs.astype(bf16)

    grad_attn = jnp.dot(
        whole.reshape(-1, whole.shape[-1]), weight, preferred_element_type=f32
    ).astype(bf16)
    grad = head_major(grad_attn.reshape(queries.shape)).reshape(heads, q_tiles, tile_len, HEAD)

    attn = jnp.einsum("hqtl,hld->hqtd", probs_lo, val_e, preferred_element_type=f32)
    delta = jnp.sum(grad.astype(f32) * attn, axis=-1, keepdims=True)
    grad_probs = jnp.einsum("hqtd,hld->hqtl", grad, val_e, preferred_element_type=f32)
    grad_scores = (probs * (grad_probs - delta) * scale).astype(bf16)
    grad_q = jnp.einsum("hqtl,hld->hqtd", grad_scores, key_e, preferred_element_type=f32)
    grad_k = jnp.einsum("hqtl,hqtd->hld", grad_scores, query, preferred_element_type=f32)
    grad_v = jnp.einsum("hqtl,hqtd->hld", probs_lo, grad, preferred_element_type=f32)

    grad_q = grad_q.astype(bf16).reshape(heads, frames * tile_rows, tile_cols, tile_len, HEAD)
    shape_e = (heads, frames * ext_r, ext_c, tile_len, HEAD)
    own_k, own_v = folded(grad_k.reshape(shape_e), grad_v.reshape(shape_e))
    return (head_minor(grad_q), head_minor(own_k.astype(bf16)), head_minor(own_v.astype(bf16)))


def solution(mesh):
    in_specs = (
        P(None, "ha", "wa", None, "tp"),
        P(None, "ha", "wa", None, "tp"),
        P(None, "ha", "wa", None, "tp"),
        P(None, "ha", "wa", None, "tp"),
        P(("ha", "wa"), "tp"),
    )
    out_specs = (
        P(None, "ha", "wa", None, "tp"),
        P(None, "ha", "wa", None, "tp"),
        P(None, "ha", "wa", None, "tp"),
    )
    return jax.shard_map(local, mesh=mesh, in_specs=in_specs, out_specs=out_specs, check_vma=False)
```

```python
import jax
import jax.numpy as jnp
from jax import lax
from jax.sharding import PartitionSpec as P

HEAD = 128


def doubling_gather(block, steps):
    sizes = {"ha": lax.axis_size("ha"), "wa": lax.axis_size("wa")}
    index = {"ha": lax.axis_index("ha"), "wa": lax.axis_index("wa")}
    buf = block
    for axis, bit in steps:
        count = sizes[axis]
        other = lax.ppermute(buf, axis, [(i, i ^ bit) for i in range(count)])
        low = (index[axis] // bit) % 2 == 0
        buf = jnp.where(low, jnp.concatenate([buf, other], 0), jnp.concatenate([other, buf], 0))
    return buf


def gather_rows(out_proj):
    ha, wa = lax.axis_size("ha"), lax.axis_size("wa")
    ha_bits = [1 << b for b in range(ha.bit_length() - 1)]
    wa_bits = [1 << b for b in range(wa.bit_length() - 1)]
    steps = [("wa", b) for b in reversed(wa_bits)] + [("ha", b) for b in reversed(ha_bits)]
    buf = doubling_gather(out_proj, steps)
    rows, cols = out_proj.shape
    order = list(reversed(steps))
    buf = buf.reshape([2] * len(steps) + [rows, cols])
    natural = [("ha", b) for b in reversed(ha_bits)] + [("wa", b) for b in reversed(wa_bits)]
    perm = [order.index(s) for s in natural] + [len(steps), len(steps) + 1]
    return buf.transpose(perm).reshape(-1, cols)


def pick(length, d):
    if d < 0:
        return slice(length - 1, length)
    if d > 0:
        return slice(0, 1)
    return slice(0, length)


def neighbour_pairs(d_r, d_c):
    ha, wa = lax.axis_size("ha"), lax.axis_size("wa")
    pairs = []
    for i in range(ha):
        for j in range(wa):
            ti, tj = i - d_r, j - d_c
            if 0 <= ti < ha and 0 <= tj < wa:
                pairs.append((i * wa + j, ti * wa + tj))
    return pairs


DIRS = [(-1, -1), (-1, 0), (-1, 1), (0, -1), (0, 1), (1, -1), (1, 0), (1, 1)]


def extended(stacked):
    _, _, rows, cols = stacked.shape[:4]
    out = jnp.pad(stacked, ((0, 0), (0, 0), (1, 1), (1, 1), (0, 0), (0, 0)))
    for d_r, d_c in DIRS:
        piece = stacked[:, :, pick(rows, d_r), pick(cols, d_c)]
        got = lax.ppermute(piece, ("ha", "wa"), neighbour_pairs(d_r, d_c))
        r0 = 0 if d_r < 0 else (rows + 1 if d_r > 0 else 1)
        c0 = 0 if d_c < 0 else (cols + 1 if d_c > 0 else 1)
        out = lax.dynamic_update_slice(out, got, (0, 0, r0, c0, 0, 0))
    return out


def passed_along(value, axis, steps):
    count = lax.axis_size(axis)
    first, last = (max(0, -steps), min(count, count - steps))
    return lax.ppermute(value, axis, [(source, source + steps) for source in range(first, last)])


def sent_back(pieces, axis, steps):
    got = passed_along(jnp.stack(pieces).astype(jnp.bfloat16), axis, steps)
    return got.astype(jnp.float32)


def folded(grad_k, grad_v):
    from_right = sent_back([grad_k[:, :, 0], grad_v[:, :, 0]], "wa", -1)
    from_left = sent_back([grad_k[:, :, -1], grad_v[:, :, -1]], "wa", 1)
    own = []
    for n, part in enumerate((grad_k, grad_v)):
        inner = part[:, :, 1:-1]
        inner = inner.at[:, :, 0:1].add(from_left[n][:, :, None])
        inner = inner.at[:, :, -1:].add(from_right[n][:, :, None])
        own.append(inner)
    from_below = sent_back([own[0][:, 0], own[1][:, 0]], "ha", -1)
    from_above = sent_back([own[0][:, -1], own[1][:, -1]], "ha", 1)
    result = []
    for n, part in enumerate(own):
        inner = part[:, 1:-1]
        inner = inner.at[:, 0:1].add(from_above[n][:, None])
        inner = inner.at[:, -1:].add(from_below[n][:, None])
        result.append(inner)
    return result[0], result[1]


def local(queries, keys, values, grad_out, out_proj):
    frames, tile_rows, tile_cols, tile_len, columns = queries.shape
    heads = columns // HEAD
    f32, bf16 = jnp.float32, jnp.bfloat16
    whole = lax.all_gather(grad_out, "tp", axis=4, tiled=True)
    weight = gather_rows(out_proj)

    def head_major(array):
        split = array.reshape(frames * tile_rows, tile_cols, tile_len, heads, HEAD)
        return jnp.transpose(split, (3, 0, 1, 2, 4))

    def head_minor(array):
        return jnp.transpose(array, (1, 2, 3, 0, 4)).reshape(queries.shape)

    ext = extended(jnp.stack([head_major(keys), head_major(values)]))
    ext_r, ext_c = tile_rows + 2, tile_cols + 2
    row_base = lax.axis_index("ha") * tile_rows
    col_base = lax.axis_index("wa") * tile_cols
    rows_all = tile_rows * lax.axis_size("ha")
    cols_all = tile_cols * lax.axis_size("wa")
    qr = jnp.arange(tile_rows, dtype=jnp.int32)
    qc = jnp.arange(tile_cols, dtype=jnp.int32)
    sr = jnp.clip(row_base + qr - 1, 0, rows_all - 3) - row_base + 1
    sc = jnp.clip(col_base + qc - 1, 0, cols_all - 3) - col_base + 1
    kr = jnp.arange(ext_r, dtype=jnp.int32)
    kc = jnp.arange(ext_c, dtype=jnp.int32)
    in_r = (kr[None, :] >= sr[:, None]) & (kr[None, :] < sr[:, None] + 3)
    in_c = (kc[None, :] >= sc[:, None]) & (kc[None, :] < sc[:, None] + 3)
    inside = in_r[:, None, :, None] & in_c[None, :, None, :]
    inside = inside.reshape(tile_rows * tile_cols, 1, ext_r * ext_c, 1)
    inside = jnp.broadcast_to(inside, (tile_rows * tile_cols, 1, ext_r * ext_c, tile_len))
    inside = inside.reshape(1, tile_rows * tile_cols, 1, ext_r * ext_c * tile_len)
    q_tiles = tile_rows * tile_cols
    keys_n = ext_r * ext_c * tile_len
    scale = HEAD ** (-0.5)

    key_e = ext[0].reshape(heads, keys_n, HEAD)
    val_e = ext[1].reshape(heads, keys_n, HEAD)
    query = head_major(queries).reshape(heads, q_tiles, tile_len, HEAD)

    scores = jnp.einsum("hqtd,hld->hqtl", query, key_e, preferred_element_type=f32) * scale
    scores = jnp.where(inside, scores, -jnp.inf)
    scores = scores - jnp.max(scores, axis=-1, keepdims=True)
    expo = jnp.exp(scores)
    probs = expo / jnp.sum(expo, axis=-1, keepdims=True)
    probs_lo = probs.astype(bf16)

    grad_attn = jnp.dot(
        whole.reshape(-1, whole.shape[-1]), weight, preferred_element_type=f32
    ).astype(bf16)
    grad = head_major(grad_attn.reshape(queries.shape)).reshape(heads, q_tiles, tile_len, HEAD)

    attn = jnp.einsum("hqtl,hld->hqtd", probs_lo, val_e, preferred_element_type=f32)
    delta = jnp.sum(grad.astype(f32) * attn, axis=-1, keepdims=True)
    grad_probs = jnp.einsum("hqtd,hld->hqtl", grad, val_e, preferred_element_type=f32)
    grad_scores = (probs * (grad_probs - delta) * scale).astype(bf16)
    grad_q = jnp.einsum("hqtl,hld->hqtd", grad_scores, key_e, preferred_element_type=f32)
    grad_k = jnp.einsum("hqtl,hqtd->hld", grad_scores, query, preferred_element_type=f32)
    grad_v = jnp.einsum("hqtl,hqtd->hld", probs_lo, grad, preferred_element_type=f32)

    grad_q = grad_q.astype(bf16).reshape(heads, frames * tile_rows, tile_cols, tile_len, HEAD)
    shape_e = (heads, frames * ext_r, ext_c, tile_len, HEAD)
    own_k, own_v = folded(grad_k.reshape(shape_e), grad_v.reshape(shape_e))
    return (head_minor(grad_q), head_minor(own_k.astype(bf16)), head_minor(own_v.astype(bf16)))


def solution(mesh):
    in_specs = (
        P(None, "ha", "wa", None, "tp"),
        P(None, "ha", "wa", None, "tp"),
        P(None, "ha", "wa", None, "tp"),
        P(None, "ha", "wa", None, "tp"),
        P(("ha", "wa"), "tp"),
    )
    out_specs = (
        P(None, "ha", "wa", None, "tp"),
        P(None, "ha", "wa", None, "tp"),
        P(None, "ha", "wa", None, "tp"),
    )
    return jax.shard_map(local, mesh=mesh, in_specs=in_specs, out_specs=out_specs, check_vma=False)
```

```python
import jax
import jax.numpy as jnp
from jax import lax
from jax.sharding import PartitionSpec as P

HEAD = 128


def doubling_gather(block, steps):
    sizes = {"ha": lax.axis_size("ha"), "wa": lax.axis_size("wa")}
    index = {"ha": lax.axis_index("ha"), "wa": lax.axis_index("wa")}
    buf = block
    for axis, bit in steps:
        count = sizes[axis]
        other = lax.ppermute(buf, axis, [(i, i ^ bit) for i in range(count)])
        low = (index[axis] // bit) % 2 == 0
        buf = jnp.where(low, jnp.concatenate([buf, other], 0), jnp.concatenate([other, buf], 0))
    return buf


def gather_rows(out_proj):
    ha, wa = lax.axis_size("ha"), lax.axis_size("wa")
    ha_bits = [1 << b for b in range(ha.bit_length() - 1)]
    wa_bits = [1 << b for b in range(wa.bit_length() - 1)]
    steps = [("wa", b) for b in reversed(wa_bits)] + [("ha", b) for b in reversed(ha_bits)]
    buf = doubling_gather(out_proj, steps)
    rows, cols = out_proj.shape
    order = list(reversed(steps))
    buf = buf.reshape([2] * len(steps) + [rows, cols])
    natural = [("ha", b) for b in reversed(ha_bits)] + [("wa", b) for b in reversed(wa_bits)]
    perm = [order.index(s) for s in natural] + [len(steps), len(steps) + 1]
    return buf.transpose(perm).reshape(-1, cols)


def pick(length, d):
    if d < 0:
        return slice(length - 1, length)
    if d > 0:
        return slice(0, 1)
    return slice(0, length)


def neighbour_pairs(d_r, d_c):
    ha, wa = lax.axis_size("ha"), lax.axis_size("wa")
    pairs = []
    for i in range(ha):
        for j in range(wa):
            ti, tj = i - d_r, j - d_c
            if 0 <= ti < ha and 0 <= tj < wa:
                pairs.append((i * wa + j, ti * wa + tj))
    return pairs


DIRS = [(-1, -1), (-1, 0), (-1, 1), (0, -1), (0, 1), (1, -1), (1, 0), (1, 1)]


def extended(stacked):
    _, _, rows, cols = stacked.shape[:4]
    out = jnp.pad(stacked, ((0, 0), (0, 0), (1, 1), (1, 1), (0, 0), (0, 0)))
    for d_r, d_c in DIRS:
        piece = stacked[:, :, pick(rows, d_r), pick(cols, d_c)]
        got = lax.ppermute(piece, ("ha", "wa"), neighbour_pairs(d_r, d_c))
        r0 = 0 if d_r < 0 else (rows + 1 if d_r > 0 else 1)
        c0 = 0 if d_c < 0 else (cols + 1 if d_c > 0 else 1)
        out = lax.dynamic_update_slice(out, got, (0, 0, r0, c0, 0, 0))
    return out


def passed_along(value, axis, steps):
    count = lax.axis_size(axis)
    first, last = (max(0, -steps), min(count, count - steps))
    return lax.ppermute(value, axis, [(source, source + steps) for source in range(first, last)])


def sent_back(pieces, axis, steps):
    got = passed_along(jnp.stack(pieces).astype(jnp.bfloat16), axis, steps)
    return got.astype(jnp.float32)


def extended_2(array, sides, width):
    for axis, dim in sides:
        peers, length = (lax.axis_size(axis), array.shape[dim])
        up = [(i, (i + 1) % peers) for i in range(peers - 1)]
        down = [(j, i) for i, j in up]
        last = lax.slice_in_dim(array, length - width, length, axis=dim)
        first = lax.slice_in_dim(array, 0, width, axis=dim)
        before = lax.ppermute(last, axis, up)
        after = lax.ppermute(first, axis, down)
        array = jnp.concatenate([before, array, after], axis=dim)
    return array


def folded(grad_k, grad_v):
    from_right = sent_back([grad_k[:, :, 0], grad_v[:, :, 0]], "wa", -1)
    from_left = sent_back([grad_k[:, :, -1], grad_v[:, :, -1]], "wa", 1)
    own = []
    for n, part in enumerate((grad_k, grad_v)):
        inner = part[:, :, 1:-1]
        inner = inner.at[:, :, 0:1].add(from_left[n][:, :, None])
        inner = inner.at[:, :, -1:].add(from_right[n][:, :, None])
        own.append(inner)
    from_below = sent_back([own[0][:, 0], own[1][:, 0]], "ha", -1)
    from_above = sent_back([own[0][:, -1], own[1][:, -1]], "ha", 1)
    result = []
    for n, part in enumerate(own):
        inner = part[:, 1:-1]
        inner = inner.at[:, 0:1].add(from_above[n][:, None])
        inner = inner.at[:, -1:].add(from_below[n][:, None])
        result.append(inner)
    return result[0], result[1]


def local(queries, keys, values, grad_out, out_proj):
    frames, tile_rows, tile_cols, tile_len, columns = queries.shape
    heads = columns // HEAD
    f32, bf16 = jnp.float32, jnp.bfloat16
    whole = lax.all_gather(grad_out, "tp", axis=4, tiled=True)
    weight = gather_rows(out_proj)

    def head_major(array):
        split = array.reshape(frames * tile_rows, tile_cols, tile_len, heads, HEAD)
        return jnp.transpose(split, (3, 0, 1, 2, 4))

    def head_minor(array):
        return jnp.transpose(array, (1, 2, 3, 0, 4)).reshape(queries.shape)

    ext = extended_2(jnp.stack([head_major(keys), head_major(values)]), (("ha", 2), ("wa", 3)), 1)
    ext_r, ext_c = tile_rows + 2, tile_cols + 2
    row_base = lax.axis_index("ha") * tile_rows
    col_base = lax.axis_index("wa") * tile_cols
    rows_all = tile_rows * lax.axis_size("ha")
    cols_all = tile_cols * lax.axis_size("wa")
    qr = jnp.arange(tile_rows, dtype=jnp.int32)
    qc = jnp.arange(tile_cols, dtype=jnp.int32)
    sr = jnp.clip(row_base + qr - 1, 0, rows_all - 3) - row_base + 1
    sc = jnp.clip(col_base + qc - 1, 0, cols_all - 3) - col_base + 1
    kr = jnp.arange(ext_r, dtype=jnp.int32)
    kc = jnp.arange(ext_c, dtype=jnp.int32)
    in_r = (kr[None, :] >= sr[:, None]) & (kr[None, :] < sr[:, None] + 3)
    in_c = (kc[None, :] >= sc[:, None]) & (kc[None, :] < sc[:, None] + 3)
    inside = in_r[:, None, :, None] & in_c[None, :, None, :]
    inside = inside.reshape(tile_rows * tile_cols, 1, ext_r * ext_c, 1)
    inside = jnp.broadcast_to(inside, (tile_rows * tile_cols, 1, ext_r * ext_c, tile_len))
    inside = inside.reshape(1, tile_rows * tile_cols, 1, ext_r * ext_c * tile_len)
    q_tiles = tile_rows * tile_cols
    keys_n = ext_r * ext_c * tile_len
    scale = HEAD ** (-0.5)

    key_e = ext[0].reshape(heads, keys_n, HEAD)
    val_e = ext[1].reshape(heads, keys_n, HEAD)
    query = head_major(queries).reshape(heads, q_tiles, tile_len, HEAD)

    scores = jnp.einsum("hqtd,hld->hqtl", query, key_e, preferred_element_type=f32) * scale
    scores = jnp.where(inside, scores, -jnp.inf)
    scores = scores - jnp.max(scores, axis=-1, keepdims=True)
    expo = jnp.exp(scores)
    probs = expo / jnp.sum(expo, axis=-1, keepdims=True)
    probs_lo = probs.astype(bf16)

    grad_attn = jnp.dot(
        whole.reshape(-1, whole.shape[-1]), weight, preferred_element_type=f32
    ).astype(bf16)
    grad = head_major(grad_attn.reshape(queries.shape)).reshape(heads, q_tiles, tile_len, HEAD)

    attn = jnp.einsum("hqtl,hld->hqtd", probs_lo, val_e, preferred_element_type=f32)
    delta = jnp.sum(grad.astype(f32) * attn, axis=-1, keepdims=True)
    grad_probs = jnp.einsum("hqtd,hld->hqtl", grad, val_e, preferred_element_type=f32)
    grad_scores = (probs * (grad_probs - delta) * scale).astype(bf16)
    grad_q = jnp.einsum("hqtl,hld->hqtd", grad_scores, key_e, preferred_element_type=f32)
    grad_k = jnp.einsum("hqtl,hqtd->hld", grad_scores, query, preferred_element_type=f32)
    grad_v = jnp.einsum("hqtl,hqtd->hld", probs_lo, grad, preferred_element_type=f32)

    grad_q = grad_q.astype(bf16).reshape(heads, frames * tile_rows, tile_cols, tile_len, HEAD)
    shape_e = (heads, frames * ext_r, ext_c, tile_len, HEAD)
    own_k, own_v = folded(grad_k.reshape(shape_e), grad_v.reshape(shape_e))
    return (head_minor(grad_q), head_minor(own_k.astype(bf16)), head_minor(own_v.astype(bf16)))


def solution(mesh):
    in_specs = (
        P(None, "ha", "wa", None, "tp"),
        P(None, "ha", "wa", None, "tp"),
        P(None, "ha", "wa", None, "tp"),
        P(None, "ha", "wa", None, "tp"),
        P(("ha", "wa"), "tp"),
    )
    out_specs = (
        P(None, "ha", "wa", None, "tp"),
        P(None, "ha", "wa", None, "tp"),
        P(None, "ha", "wa", None, "tp"),
    )
    return jax.shard_map(local, mesh=mesh, in_specs=in_specs, out_specs=out_specs, check_vma=False)
```

```python
import jax
import jax.numpy as jnp
from jax import lax
from jax.sharding import PartitionSpec as P

HEAD = 128


def doubling_gather(block, steps):
    sizes = {"ha": lax.axis_size("ha"), "wa": lax.axis_size("wa")}
    index = {"ha": lax.axis_index("ha"), "wa": lax.axis_index("wa")}
    buf = block
    for axis, bit in steps:
        count = sizes[axis]
        other = lax.ppermute(buf, axis, [(i, i ^ bit) for i in range(count)])
        low = (index[axis] // bit) % 2 == 0
        buf = jnp.where(low, jnp.concatenate([buf, other], 0), jnp.concatenate([other, buf], 0))
    return buf


def gather_rows(out_proj):
    ha, wa = lax.axis_size("ha"), lax.axis_size("wa")
    ha_bits = [1 << b for b in range(ha.bit_length() - 1)]
    wa_bits = [1 << b for b in range(wa.bit_length() - 1)]
    steps = [("wa", b) for b in reversed(wa_bits)] + [("ha", b) for b in reversed(ha_bits)]
    buf = doubling_gather(out_proj, steps)
    rows, cols = out_proj.shape
    order = list(reversed(steps))
    buf = buf.reshape([2] * len(steps) + [rows, cols])
    natural = [("ha", b) for b in reversed(ha_bits)] + [("wa", b) for b in reversed(wa_bits)]
    perm = [order.index(s) for s in natural] + [len(steps), len(steps) + 1]
    return buf.transpose(perm).reshape(-1, cols)


def pick(length, d):
    if d < 0:
        return slice(length - 1, length)
    if d > 0:
        return slice(0, 1)
    return slice(0, length)


def neighbour_pairs(d_r, d_c):
    ha, wa = lax.axis_size("ha"), lax.axis_size("wa")
    pairs = []
    for i in range(ha):
        for j in range(wa):
            ti, tj = i - d_r, j - d_c
            if 0 <= ti < ha and 0 <= tj < wa:
                pairs.append((i * wa + j, ti * wa + tj))
    return pairs


DIRS = [(-1, -1), (-1, 0), (-1, 1), (0, -1), (0, 1), (1, -1), (1, 0), (1, 1)]


def extended(stacked):
    _, _, rows, cols = stacked.shape[:4]
    out = jnp.pad(stacked, ((0, 0), (0, 0), (1, 1), (1, 1), (0, 0), (0, 0)))
    for d_r, d_c in DIRS:
        piece = stacked[:, :, pick(rows, d_r), pick(cols, d_c)]
        got = lax.ppermute(piece, ("ha", "wa"), neighbour_pairs(d_r, d_c))
        r0 = 0 if d_r < 0 else (rows + 1 if d_r > 0 else 1)
        c0 = 0 if d_c < 0 else (cols + 1 if d_c > 0 else 1)
        out = lax.dynamic_update_slice(out, got, (0, 0, r0, c0, 0, 0))
    return out


def passed_along(value, axis, steps):
    count = lax.axis_size(axis)
    first, last = (max(0, -steps), min(count, count - steps))
    return lax.ppermute(value, axis, [(source, source + steps) for source in range(first, last)])


def sent_back(pieces, axis, steps):
    got = passed_along(jnp.stack(pieces).astype(jnp.bfloat16), axis, steps)
    return got.astype(jnp.float32)


def extended_2(array, sides, width):
    for axis, dim in sides:
        peers, length = (lax.axis_size(axis), array.shape[dim])
        up = [(i, (i + 1) % peers) for i in range(peers - 1)]
        down = [(j, i) for i, j in up]
        last = lax.slice_in_dim(array, length - width, length, axis=dim)
        first = lax.slice_in_dim(array, 0, width, axis=dim)
        before = lax.ppermute(last, axis, up)
        after = lax.ppermute(first, axis, down)
        array = jnp.concatenate([before, array, after], axis=dim)
    return array


def folded(grad_k, grad_v):
    from_below = sent_back([grad_k[:, 0], grad_v[:, 0]], "ha", -1)
    from_above = sent_back([grad_k[:, -1], grad_v[:, -1]], "ha", 1)
    own = []
    for n, part in enumerate((grad_k, grad_v)):
        inner = part[:, 1:-1]
        inner = inner.at[:, 0:1].add(from_above[n][:, None])
        inner = inner.at[:, -1:].add(from_below[n][:, None])
        own.append(inner)
    from_right = sent_back([own[0][:, :, 0], own[1][:, :, 0]], "wa", -1)
    from_left = sent_back([own[0][:, :, -1], own[1][:, :, -1]], "wa", 1)
    result = []
    for n, part in enumerate(own):
        inner = part[:, :, 1:-1]
        inner = inner.at[:, :, 0:1].add(from_left[n][:, :, None])
        inner = inner.at[:, :, -1:].add(from_right[n][:, :, None])
        result.append(inner)
    return result[0], result[1]


def local(queries, keys, values, grad_out, out_proj):
    frames, tile_rows, tile_cols, tile_len, columns = queries.shape
    heads = columns // HEAD
    f32, bf16 = jnp.float32, jnp.bfloat16
    whole = lax.all_gather(grad_out, "tp", axis=4, tiled=True)
    weight = gather_rows(out_proj)

    def head_major(array):
        split = array.reshape(frames * tile_rows, tile_cols, tile_len, heads, HEAD)
        return jnp.transpose(split, (3, 0, 1, 2, 4))

    def head_minor(array):
        return jnp.transpose(array, (1, 2, 3, 0, 4)).reshape(queries.shape)

    ext = extended_2(jnp.stack([head_major(keys), head_major(values)]), (("wa", 3), ("ha", 2)), 1)
    ext_r, ext_c = tile_rows + 2, tile_cols + 2
    row_base = lax.axis_index("ha") * tile_rows
    col_base = lax.axis_index("wa") * tile_cols
    rows_all = tile_rows * lax.axis_size("ha")
    cols_all = tile_cols * lax.axis_size("wa")
    qr = jnp.arange(tile_rows, dtype=jnp.int32)
    qc = jnp.arange(tile_cols, dtype=jnp.int32)
    sr = jnp.clip(row_base + qr - 1, 0, rows_all - 3) - row_base + 1
    sc = jnp.clip(col_base + qc - 1, 0, cols_all - 3) - col_base + 1
    kr = jnp.arange(ext_r, dtype=jnp.int32)
    kc = jnp.arange(ext_c, dtype=jnp.int32)
    in_r = (kr[None, :] >= sr[:, None]) & (kr[None, :] < sr[:, None] + 3)
    in_c = (kc[None, :] >= sc[:, None]) & (kc[None, :] < sc[:, None] + 3)
    inside = in_r[:, None, :, None] & in_c[None, :, None, :]
    inside = inside.reshape(tile_rows * tile_cols, 1, ext_r * ext_c, 1)
    inside = jnp.broadcast_to(inside, (tile_rows * tile_cols, 1, ext_r * ext_c, tile_len))
    inside = inside.reshape(1, tile_rows * tile_cols, 1, ext_r * ext_c * tile_len)
    q_tiles = tile_rows * tile_cols
    keys_n = ext_r * ext_c * tile_len
    scale = HEAD ** (-0.5)

    key_e = ext[0].reshape(heads, keys_n, HEAD)
    val_e = ext[1].reshape(heads, keys_n, HEAD)
    query = head_major(queries).reshape(heads, q_tiles, tile_len, HEAD)

    scores = jnp.einsum("hqtd,hld->hqtl", query, key_e, preferred_element_type=f32) * scale
    scores = jnp.where(inside, scores, -jnp.inf)
    scores = scores - jnp.max(scores, axis=-1, keepdims=True)
    expo = jnp.exp(scores)
    probs = expo / jnp.sum(expo, axis=-1, keepdims=True)
    probs_lo = probs.astype(bf16)

    grad_attn = jnp.dot(
        whole.reshape(-1, whole.shape[-1]), weight, preferred_element_type=f32
    ).astype(bf16)
    grad = head_major(grad_attn.reshape(queries.shape)).reshape(heads, q_tiles, tile_len, HEAD)

    attn = jnp.einsum("hqtl,hld->hqtd", probs_lo, val_e, preferred_element_type=f32)
    delta = jnp.sum(grad.astype(f32) * attn, axis=-1, keepdims=True)
    grad_probs = jnp.einsum("hqtd,hld->hqtl", grad, val_e, preferred_element_type=f32)
    grad_scores = (probs * (grad_probs - delta) * scale).astype(bf16)
    grad_q = jnp.einsum("hqtl,hld->hqtd", grad_scores, key_e, preferred_element_type=f32)
    grad_k = jnp.einsum("hqtl,hqtd->hld", grad_scores, query, preferred_element_type=f32)
    grad_v = jnp.einsum("hqtl,hqtd->hld", probs_lo, grad, preferred_element_type=f32)

    grad_q = grad_q.astype(bf16).reshape(heads, frames * tile_rows, tile_cols, tile_len, HEAD)
    shape_e = (heads, frames * ext_r, ext_c, tile_len, HEAD)
    own_k, own_v = folded(grad_k.reshape(shape_e), grad_v.reshape(shape_e))
    return (head_minor(grad_q), head_minor(own_k.astype(bf16)), head_minor(own_v.astype(bf16)))


def solution(mesh):
    in_specs = (
        P(None, "ha", "wa", None, "tp"),
        P(None, "ha", "wa", None, "tp"),
        P(None, "ha", "wa", None, "tp"),
        P(None, "ha", "wa", None, "tp"),
        P(("ha", "wa"), "tp"),
    )
    out_specs = (
        P(None, "ha", "wa", None, "tp"),
        P(None, "ha", "wa", None, "tp"),
        P(None, "ha", "wa", None, "tp"),
    )
    return jax.shard_map(local, mesh=mesh, in_specs=in_specs, out_specs=out_specs, check_vma=False)
```

```python
import jax
import jax.numpy as jnp
from jax import lax
from jax.sharding import PartitionSpec as P

HEAD = 128


def gather_rows(out_proj):
    rows, cols = out_proj.shape
    bits = []
    for axis in ("ha", "wa"):
        size = lax.axis_size(axis)
        bits += [(axis, 1 << b) for b in reversed(range(size.bit_length() - 1))]
    index = {"ha": lax.axis_index("ha"), "wa": lax.axis_index("wa")}
    mine = [(index[axis] // bit) % 2 for axis, bit in bits]
    zero = jnp.zeros((), jnp.int32)
    buf = jnp.zeros([2] * len(bits) + [rows, cols], out_proj.dtype)
    start = mine + [zero, zero]
    buf = lax.dynamic_update_slice(buf, out_proj.reshape([1] * len(bits) + [rows, cols]), start)
    done = []
    steps = [b for b in bits if b[0] == "wa"] + [b for b in bits if b[0] == "ha"]
    for axis, bit in steps:
        k = bits.index((axis, bit))
        sizes = [2 if n in done else 1 for n in range(len(bits))] + [rows, cols]
        start = [zero if n in done else mine[n] for n in range(len(bits))] + [zero, zero]
        box = lax.dynamic_slice(buf, start, sizes)
        count = lax.axis_size(axis)
        got = lax.ppermute(box, axis, [(i, i ^ bit) for i in range(count)])
        start[k] = 1 - mine[k]
        buf = lax.dynamic_update_slice(buf, got, start)
        done.append(k)
    return buf.reshape(-1, cols)


def pick(length, d):
    if d < 0:
        return slice(length - 1, length)
    if d > 0:
        return slice(0, 1)
    return slice(0, length)


def neighbour_pairs(d_r, d_c):
    ha, wa = lax.axis_size("ha"), lax.axis_size("wa")
    pairs = []
    for i in range(ha):
        for j in range(wa):
            ti, tj = i - d_r, j - d_c
            if 0 <= ti < ha and 0 <= tj < wa:
                pairs.append((i * wa + j, ti * wa + tj))
    return pairs


DIRS = [(-1, -1), (-1, 0), (-1, 1), (0, -1), (0, 1), (1, -1), (1, 0), (1, 1)]


def extended(stacked):
    _, _, rows, cols = stacked.shape[:4]
    out = jnp.pad(stacked, ((0, 0), (0, 0), (1, 1), (1, 1), (0, 0), (0, 0)))
    for d_r, d_c in DIRS:
        piece = stacked[:, :, pick(rows, d_r), pick(cols, d_c)]
        got = lax.ppermute(piece, ("ha", "wa"), neighbour_pairs(d_r, d_c))
        r0 = 0 if d_r < 0 else (rows + 1 if d_r > 0 else 1)
        c0 = 0 if d_c < 0 else (cols + 1 if d_c > 0 else 1)
        out = lax.dynamic_update_slice(out, got, (0, 0, r0, c0, 0, 0))
    return out


def passed_along(value, axis, steps):
    count = lax.axis_size(axis)
    first, last = (max(0, -steps), min(count, count - steps))
    return lax.ppermute(value, axis, [(source, source + steps) for source in range(first, last)])


def sent_back(pieces, axis, steps):
    got = passed_along(jnp.stack(pieces).astype(jnp.bfloat16), axis, steps)
    return got.astype(jnp.float32)


def extended_2(array, sides, width):
    for axis, dim in sides:
        peers, length = (lax.axis_size(axis), array.shape[dim])
        up = [(i, (i + 1) % peers) for i in range(peers - 1)]
        down = [(j, i) for i, j in up]
        last = lax.slice_in_dim(array, length - width, length, axis=dim)
        first = lax.slice_in_dim(array, 0, width, axis=dim)
        before = lax.ppermute(last, axis, up)
        after = lax.ppermute(first, axis, down)
        array = jnp.concatenate([before, array, after], axis=dim)
    return array


def folded(grad_k, grad_v):
    from_below = sent_back([grad_k[:, 0], grad_v[:, 0]], "ha", -1)
    from_above = sent_back([grad_k[:, -1], grad_v[:, -1]], "ha", 1)
    own = []
    for n, part in enumerate((grad_k, grad_v)):
        inner = part[:, 1:-1]
        inner = inner.at[:, 0:1].add(from_above[n][:, None])
        inner = inner.at[:, -1:].add(from_below[n][:, None])
        own.append(inner)
    from_right = sent_back([own[0][:, :, 0], own[1][:, :, 0]], "wa", -1)
    from_left = sent_back([own[0][:, :, -1], own[1][:, :, -1]], "wa", 1)
    result = []
    for n, part in enumerate(own):
        inner = part[:, :, 1:-1]
        inner = inner.at[:, :, 0:1].add(from_left[n][:, :, None])
        inner = inner.at[:, :, -1:].add(from_right[n][:, :, None])
        result.append(inner)
    return result[0], result[1]


def local(queries, keys, values, grad_out, out_proj):
    frames, tile_rows, tile_cols, tile_len, columns = queries.shape
    heads = columns // HEAD
    f32, bf16 = jnp.float32, jnp.bfloat16
    whole = lax.all_gather(grad_out, "tp", axis=4, tiled=True)
    weight = gather_rows(out_proj)

    def head_major(array):
        split = array.reshape(frames * tile_rows, tile_cols, tile_len, heads, HEAD)
        return jnp.transpose(split, (3, 0, 1, 2, 4))

    def head_minor(array):
        return jnp.transpose(array, (1, 2, 3, 0, 4)).reshape(queries.shape)

    ext = extended_2(jnp.stack([head_major(keys), head_major(values)]), (("wa", 3), ("ha", 2)), 1)
    ext_r, ext_c = tile_rows + 2, tile_cols + 2
    row_base = lax.axis_index("ha") * tile_rows
    col_base = lax.axis_index("wa") * tile_cols
    rows_all = tile_rows * lax.axis_size("ha")
    cols_all = tile_cols * lax.axis_size("wa")
    qr = jnp.arange(tile_rows, dtype=jnp.int32)
    qc = jnp.arange(tile_cols, dtype=jnp.int32)
    sr = jnp.clip(row_base + qr - 1, 0, rows_all - 3) - row_base + 1
    sc = jnp.clip(col_base + qc - 1, 0, cols_all - 3) - col_base + 1
    kr = jnp.arange(ext_r, dtype=jnp.int32)
    kc = jnp.arange(ext_c, dtype=jnp.int32)
    in_r = (kr[None, :] >= sr[:, None]) & (kr[None, :] < sr[:, None] + 3)
    in_c = (kc[None, :] >= sc[:, None]) & (kc[None, :] < sc[:, None] + 3)
    inside = in_r[:, None, :, None] & in_c[None, :, None, :]
    inside = inside.reshape(tile_rows * tile_cols, 1, ext_r * ext_c, 1)
    inside = jnp.broadcast_to(inside, (tile_rows * tile_cols, 1, ext_r * ext_c, tile_len))
    inside = inside.reshape(1, tile_rows * tile_cols, 1, ext_r * ext_c * tile_len)
    q_tiles = tile_rows * tile_cols
    keys_n = ext_r * ext_c * tile_len
    scale = HEAD ** (-0.5)

    key_e = ext[0].reshape(heads, keys_n, HEAD)
    val_e = ext[1].reshape(heads, keys_n, HEAD)
    query = head_major(queries).reshape(heads, q_tiles, tile_len, HEAD)

    scores = jnp.einsum("hqtd,hld->hqtl", query, key_e, preferred_element_type=f32) * scale
    scores = jnp.where(inside, scores, -jnp.inf)
    scores = scores - jnp.max(scores, axis=-1, keepdims=True)
    expo = jnp.exp(scores)
    probs = expo / jnp.sum(expo, axis=-1, keepdims=True)
    probs_lo = probs.astype(bf16)

    grad_attn = jnp.dot(
        whole.reshape(-1, whole.shape[-1]), weight, preferred_element_type=f32
    ).astype(bf16)
    grad = head_major(grad_attn.reshape(queries.shape)).reshape(heads, q_tiles, tile_len, HEAD)

    attn = jnp.einsum("hqtl,hld->hqtd", probs_lo, val_e, preferred_element_type=f32)
    delta = jnp.sum(grad.astype(f32) * attn, axis=-1, keepdims=True)
    grad_probs = jnp.einsum("hqtd,hld->hqtl", grad, val_e, preferred_element_type=f32)
    grad_scores = (probs * (grad_probs - delta) * scale).astype(bf16)
    grad_q = jnp.einsum("hqtl,hld->hqtd", grad_scores, key_e, preferred_element_type=f32)
    grad_k = jnp.einsum("hqtl,hqtd->hld", grad_scores, query, preferred_element_type=f32)
    grad_v = jnp.einsum("hqtl,hqtd->hld", probs_lo, grad, preferred_element_type=f32)

    grad_q = grad_q.astype(bf16).reshape(heads, frames * tile_rows, tile_cols, tile_len, HEAD)
    shape_e = (heads, frames * ext_r, ext_c, tile_len, HEAD)
    own_k, own_v = folded(grad_k.reshape(shape_e), grad_v.reshape(shape_e))
    return (head_minor(grad_q), head_minor(own_k.astype(bf16)), head_minor(own_v.astype(bf16)))


def solution(mesh):
    in_specs = (
        P(None, "ha", "wa", None, "tp"),
        P(None, "ha", "wa", None, "tp"),
        P(None, "ha", "wa", None, "tp"),
        P(None, "ha", "wa", None, "tp"),
        P(("ha", "wa"), "tp"),
    )
    out_specs = (
        P(None, "ha", "wa", None, "tp"),
        P(None, "ha", "wa", None, "tp"),
        P(None, "ha", "wa", None, "tp"),
    )
    return jax.shard_map(local, mesh=mesh, in_specs=in_specs, out_specs=out_specs, check_vma=False)
```

```python
import jax
import jax.numpy as jnp
from jax import lax
from jax.sharding import PartitionSpec as P

HEAD = 128


def doubling_gather(block, steps):
    sizes = {"ha": lax.axis_size("ha"), "wa": lax.axis_size("wa")}
    index = {"ha": lax.axis_index("ha"), "wa": lax.axis_index("wa")}
    buf = block
    for axis, bit in steps:
        count = sizes[axis]
        other = lax.ppermute(buf, axis, [(i, i ^ bit) for i in range(count)])
        low = (index[axis] // bit) % 2 == 0
        buf = jnp.where(low, jnp.concatenate([buf, other], 0), jnp.concatenate([other, buf], 0))
    return buf


def gather_rows(out_proj):
    ha, wa = lax.axis_size("ha"), lax.axis_size("wa")
    ha_bits = [1 << b for b in range(ha.bit_length() - 1)]
    wa_bits = [1 << b for b in range(wa.bit_length() - 1)]
    steps = [("wa", b) for b in reversed(wa_bits)] + [("ha", b) for b in reversed(ha_bits)]
    buf = doubling_gather(out_proj, steps)
    rows, cols = out_proj.shape
    order = list(reversed(steps))
    buf = buf.reshape([2] * len(steps) + [rows, cols])
    natural = [("ha", b) for b in reversed(ha_bits)] + [("wa", b) for b in reversed(wa_bits)]
    perm = [order.index(s) for s in natural] + [len(steps), len(steps) + 1]
    return buf.transpose(perm).reshape(-1, cols)


def pick(length, d):
    if d < 0:
        return slice(length - 1, length)
    if d > 0:
        return slice(0, 1)
    return slice(0, length)


def neighbour_pairs(d_r, d_c):
    ha, wa = lax.axis_size("ha"), lax.axis_size("wa")
    pairs = []
    for i in range(ha):
        for j in range(wa):
            ti, tj = i - d_r, j - d_c
            if 0 <= ti < ha and 0 <= tj < wa:
                pairs.append((i * wa + j, ti * wa + tj))
    return pairs


DIRS = [(-1, -1), (-1, 0), (-1, 1), (0, -1), (0, 1), (1, -1), (1, 0), (1, 1)]


def extended(stacked):
    _, _, rows, cols = stacked.shape[:4]
    out = jnp.pad(stacked, ((0, 0), (0, 0), (1, 1), (1, 1), (0, 0), (0, 0)))
    for d_r, d_c in DIRS:
        piece = stacked[:, :, pick(rows, d_r), pick(cols, d_c)]
        got = lax.ppermute(piece, ("ha", "wa"), neighbour_pairs(d_r, d_c))
        r0 = 0 if d_r < 0 else (rows + 1 if d_r > 0 else 1)
        c0 = 0 if d_c < 0 else (cols + 1 if d_c > 0 else 1)
        out = lax.dynamic_update_slice(out, got, (0, 0, r0, c0, 0, 0))
    return out


def passed_along(value, axis, steps):
    count = lax.axis_size(axis)
    first, last = (max(0, -steps), min(count, count - steps))
    return lax.ppermute(value, axis, [(source, source + steps) for source in range(first, last)])


def sent_back(pieces, axis, steps):
    got = passed_along(jnp.stack(pieces).astype(jnp.bfloat16), axis, steps)
    return got.astype(jnp.float32)


def extended_2(array, sides, width):
    for axis, dim in sides:
        peers, length = (lax.axis_size(axis), array.shape[dim])
        up = [(i, (i + 1) % peers) for i in range(peers - 1)]
        down = [(j, i) for i, j in up]
        last = lax.slice_in_dim(array, length - width, length, axis=dim)
        first = lax.slice_in_dim(array, 0, width, axis=dim)
        before = lax.ppermute(last, axis, up)
        after = lax.ppermute(first, axis, down)
        array = jnp.concatenate([before, array, after], axis=dim)
    return array


def folded(grad_k, grad_v):
    from_below = sent_back([grad_k[:, 0], grad_v[:, 0]], "ha", -1)
    from_above = sent_back([grad_k[:, -1], grad_v[:, -1]], "ha", 1)
    own = []
    for n, part in enumerate((grad_k, grad_v)):
        inner = part[:, 1:-1]
        inner = inner.at[:, 0:1].add(from_above[n][:, None])
        inner = inner.at[:, -1:].add(from_below[n][:, None])
        own.append(inner)
    from_right = sent_back([own[0][:, :, 0], own[1][:, :, 0]], "wa", -1)
    from_left = sent_back([own[0][:, :, -1], own[1][:, :, -1]], "wa", 1)
    result = []
    for n, part in enumerate(own):
        inner = part[:, :, 1:-1]
        inner = inner.at[:, :, 0:1].add(from_left[n][:, :, None])
        inner = inner.at[:, :, -1:].add(from_right[n][:, :, None])
        result.append(inner)
    return result[0], result[1]


def local(queries, keys, values, grad_out, out_proj):
    frames, tile_rows, tile_cols, tile_len, columns = queries.shape
    heads = columns // HEAD
    f32, bf16 = jnp.float32, jnp.bfloat16
    whole = lax.all_gather(grad_out, "tp", axis=4, tiled=True)

    def head_major(array):
        split = array.reshape(frames * tile_rows, tile_cols, tile_len, heads, HEAD)
        return jnp.transpose(split, (3, 0, 1, 2, 4))

    def head_minor(array):
        return jnp.transpose(array, (1, 2, 3, 0, 4)).reshape(queries.shape)

    ext = extended_2(jnp.stack([head_major(keys), head_major(values)]), (("wa", 3), ("ha", 2)), 1)
    ext, out_proj = lax.optimization_barrier((ext, out_proj))
    weight = gather_rows(out_proj)
    ext_r, ext_c = tile_rows + 2, tile_cols + 2
    row_base = lax.axis_index("ha") * tile_rows
    col_base = lax.axis_index("wa") * tile_cols
    rows_all = tile_rows * lax.axis_size("ha")
    cols_all = tile_cols * lax.axis_size("wa")
    qr = jnp.arange(tile_rows, dtype=jnp.int32)
    qc = jnp.arange(tile_cols, dtype=jnp.int32)
    sr = jnp.clip(row_base + qr - 1, 0, rows_all - 3) - row_base + 1
    sc = jnp.clip(col_base + qc - 1, 0, cols_all - 3) - col_base + 1
    kr = jnp.arange(ext_r, dtype=jnp.int32)
    kc = jnp.arange(ext_c, dtype=jnp.int32)
    in_r = (kr[None, :] >= sr[:, None]) & (kr[None, :] < sr[:, None] + 3)
    in_c = (kc[None, :] >= sc[:, None]) & (kc[None, :] < sc[:, None] + 3)
    inside = in_r[:, None, :, None] & in_c[None, :, None, :]
    inside = inside.reshape(tile_rows * tile_cols, 1, ext_r * ext_c, 1)
    inside = jnp.broadcast_to(inside, (tile_rows * tile_cols, 1, ext_r * ext_c, tile_len))
    inside = inside.reshape(1, tile_rows * tile_cols, 1, ext_r * ext_c * tile_len)
    q_tiles = tile_rows * tile_cols
    keys_n = ext_r * ext_c * tile_len
    scale = HEAD ** (-0.5)

    key_e = ext[0].reshape(heads, keys_n, HEAD)
    val_e = ext[1].reshape(heads, keys_n, HEAD)
    query = head_major(queries).reshape(heads, q_tiles, tile_len, HEAD)

    scores = jnp.einsum("hqtd,hld->hqtl", query, key_e, preferred_element_type=f32) * scale
    scores = jnp.where(inside, scores, -jnp.inf)
    scores = scores - jnp.max(scores, axis=-1, keepdims=True)
    expo = jnp.exp(scores)
    probs = expo / jnp.sum(expo, axis=-1, keepdims=True)
    probs_lo = probs.astype(bf16)

    grad_attn = jnp.dot(
        whole.reshape(-1, whole.shape[-1]), weight, preferred_element_type=f32
    ).astype(bf16)
    grad = head_major(grad_attn.reshape(queries.shape)).reshape(heads, q_tiles, tile_len, HEAD)

    attn = jnp.einsum("hqtl,hld->hqtd", probs_lo, val_e, preferred_element_type=f32)
    delta = jnp.sum(grad.astype(f32) * attn, axis=-1, keepdims=True)
    grad_probs = jnp.einsum("hqtd,hld->hqtl", grad, val_e, preferred_element_type=f32)
    grad_scores = (probs * (grad_probs - delta) * scale).astype(bf16)
    grad_q = jnp.einsum("hqtl,hld->hqtd", grad_scores, key_e, preferred_element_type=f32)
    grad_k = jnp.einsum("hqtl,hqtd->hld", grad_scores, query, preferred_element_type=f32)
    grad_v = jnp.einsum("hqtl,hqtd->hld", probs_lo, grad, preferred_element_type=f32)

    grad_q = grad_q.astype(bf16).reshape(heads, frames * tile_rows, tile_cols, tile_len, HEAD)
    shape_e = (heads, frames * ext_r, ext_c, tile_len, HEAD)
    own_k, own_v = folded(grad_k.reshape(shape_e), grad_v.reshape(shape_e))
    return (head_minor(grad_q), head_minor(own_k.astype(bf16)), head_minor(own_v.astype(bf16)))


def solution(mesh):
    in_specs = (
        P(None, "ha", "wa", None, "tp"),
        P(None, "ha", "wa", None, "tp"),
        P(None, "ha", "wa", None, "tp"),
        P(None, "ha", "wa", None, "tp"),
        P(("ha", "wa"), "tp"),
    )
    out_specs = (
        P(None, "ha", "wa", None, "tp"),
        P(None, "ha", "wa", None, "tp"),
        P(None, "ha", "wa", None, "tp"),
    )
    return jax.shard_map(local, mesh=mesh, in_specs=in_specs, out_specs=out_specs, check_vma=False)
```

```python
import jax
import jax.numpy as jnp
from jax import lax
from jax.sharding import PartitionSpec as P

HEAD = 128


def doubling_gather(block, steps):
    sizes = {"ha": lax.axis_size("ha"), "wa": lax.axis_size("wa")}
    index = {"ha": lax.axis_index("ha"), "wa": lax.axis_index("wa")}
    buf = block
    for axis, bit in steps:
        count = sizes[axis]
        other = lax.ppermute(buf, axis, [(i, i ^ bit) for i in range(count)])
        low = (index[axis] // bit) % 2 == 0
        buf = jnp.where(low, jnp.concatenate([buf, other], 0), jnp.concatenate([other, buf], 0))
    return buf


def gather_rows(out_proj):
    ha, wa = lax.axis_size("ha"), lax.axis_size("wa")
    ha_bits = [1 << b for b in range(ha.bit_length() - 1)]
    wa_bits = [1 << b for b in range(wa.bit_length() - 1)]
    steps = [("wa", b) for b in reversed(wa_bits)] + [("ha", b) for b in reversed(ha_bits)]
    buf = doubling_gather(out_proj, steps)
    rows, cols = out_proj.shape
    order = list(reversed(steps))
    buf = buf.reshape([2] * len(steps) + [rows, cols])
    natural = [("ha", b) for b in reversed(ha_bits)] + [("wa", b) for b in reversed(wa_bits)]
    perm = [order.index(s) for s in natural] + [len(steps), len(steps) + 1]
    return buf.transpose(perm).reshape(-1, cols)


def pick(length, d):
    if d < 0:
        return slice(length - 1, length)
    if d > 0:
        return slice(0, 1)
    return slice(0, length)


def neighbour_pairs(d_r, d_c):
    ha, wa = lax.axis_size("ha"), lax.axis_size("wa")
    pairs = []
    for i in range(ha):
        for j in range(wa):
            ti, tj = i - d_r, j - d_c
            if 0 <= ti < ha and 0 <= tj < wa:
                pairs.append((i * wa + j, ti * wa + tj))
    return pairs


DIRS = [(-1, -1), (-1, 0), (-1, 1), (0, -1), (0, 1), (1, -1), (1, 0), (1, 1)]


def extended(stacked):
    _, _, rows, cols = stacked.shape[:4]
    out = jnp.pad(stacked, ((0, 0), (0, 0), (1, 1), (1, 1), (0, 0), (0, 0)))
    for d_r, d_c in DIRS:
        piece = stacked[:, :, pick(rows, d_r), pick(cols, d_c)]
        got = lax.ppermute(piece, ("ha", "wa"), neighbour_pairs(d_r, d_c))
        r0 = 0 if d_r < 0 else (rows + 1 if d_r > 0 else 1)
        c0 = 0 if d_c < 0 else (cols + 1 if d_c > 0 else 1)
        out = lax.dynamic_update_slice(out, got, (0, 0, r0, c0, 0, 0))
    return out


def passed_along(value, axis, steps):
    count = lax.axis_size(axis)
    first, last = (max(0, -steps), min(count, count - steps))
    return lax.ppermute(value, axis, [(source, source + steps) for source in range(first, last)])


def sent_back(pieces, axis, steps):
    got = passed_along(jnp.stack(pieces).astype(jnp.bfloat16), axis, steps)
    return got.astype(jnp.float32)


def extended_2(array, sides, width):
    for axis, dim in sides:
        peers, length = (lax.axis_size(axis), array.shape[dim])
        up = [(i, (i + 1) % peers) for i in range(peers - 1)]
        down = [(j, i) for i, j in up]
        last = lax.slice_in_dim(array, length - width, length, axis=dim)
        first = lax.slice_in_dim(array, 0, width, axis=dim)
        before = lax.ppermute(last, axis, up)
        after = lax.ppermute(first, axis, down)
        array = jnp.concatenate([before, array, after], axis=dim)
    return array


def folded(grad_k, grad_v):
    from_below = sent_back([grad_k[:, 0], grad_v[:, 0]], "ha", -1)
    from_above = sent_back([grad_k[:, -1], grad_v[:, -1]], "ha", 1)
    own = []
    for n, part in enumerate((grad_k, grad_v)):
        inner = part[:, 1:-1]
        inner = inner.at[:, 0:1].add(from_above[n][:, None])
        inner = inner.at[:, -1:].add(from_below[n][:, None])
        own.append(inner)
    from_right = sent_back([own[0][:, :, 0], own[1][:, :, 0]], "wa", -1)
    from_left = sent_back([own[0][:, :, -1], own[1][:, :, -1]], "wa", 1)
    result = []
    for n, part in enumerate(own):
        inner = part[:, :, 1:-1]
        inner = inner.at[:, :, 0:1].add(from_left[n][:, :, None])
        inner = inner.at[:, :, -1:].add(from_right[n][:, :, None])
        result.append(inner)
    return result[0], result[1]


def local(queries, keys, values, grad_out, out_proj):
    frames, tile_rows, tile_cols, tile_len, columns = queries.shape
    heads = columns // HEAD
    f32, bf16 = jnp.float32, jnp.bfloat16
    whole = lax.all_gather(grad_out, "tp", axis=4, tiled=True)
    weight = gather_rows(out_proj)

    def head_major(array):
        split = array.reshape(frames * tile_rows, tile_cols, tile_len, heads, HEAD)
        return jnp.transpose(split, (3, 0, 1, 2, 4))

    def head_minor(array):
        return jnp.transpose(array, (1, 2, 3, 0, 4)).reshape(queries.shape)

    ext = extended_2(jnp.stack([head_major(keys), head_major(values)]), (("ha", 2), ("wa", 3)), 1)
    ext_r, ext_c = tile_rows + 2, tile_cols + 2
    row_base = lax.axis_index("ha") * tile_rows
    col_base = lax.axis_index("wa") * tile_cols
    rows_all = tile_rows * lax.axis_size("ha")
    cols_all = tile_cols * lax.axis_size("wa")
    qr = jnp.arange(tile_rows, dtype=jnp.int32)
    qc = jnp.arange(tile_cols, dtype=jnp.int32)
    sr = jnp.clip(row_base + qr - 1, 0, rows_all - 3) - row_base + 1
    sc = jnp.clip(col_base + qc - 1, 0, cols_all - 3) - col_base + 1
    kr = jnp.arange(ext_r, dtype=jnp.int32)
    kc = jnp.arange(ext_c, dtype=jnp.int32)
    in_r = (kr[None, :] >= sr[:, None]) & (kr[None, :] < sr[:, None] + 3)
    in_c = (kc[None, :] >= sc[:, None]) & (kc[None, :] < sc[:, None] + 3)
    inside = in_r[:, None, :, None] & in_c[None, :, None, :]
    inside = inside.reshape(tile_rows * tile_cols, 1, ext_r * ext_c, 1)
    inside = jnp.broadcast_to(inside, (tile_rows * tile_cols, 1, ext_r * ext_c, tile_len))
    inside = inside.reshape(1, tile_rows * tile_cols, 1, ext_r * ext_c * tile_len)
    q_tiles = tile_rows * tile_cols
    keys_n = ext_r * ext_c * tile_len
    scale = HEAD ** (-0.5)

    key_e = ext[0].reshape(heads, keys_n, HEAD)
    val_e = ext[1].reshape(heads, keys_n, HEAD)
    query = head_major(queries).reshape(heads, q_tiles, tile_len, HEAD)

    scores = jnp.einsum("hqtd,hld->hqtl", query, key_e, preferred_element_type=f32) * scale
    scores = jnp.where(inside, scores, -jnp.inf)
    scores = scores - jnp.max(scores, axis=-1, keepdims=True)
    expo = jnp.exp(scores)
    probs = expo / jnp.sum(expo, axis=-1, keepdims=True)
    probs_lo = probs.astype(bf16)

    grad_attn = jnp.dot(
        whole.reshape(-1, whole.shape[-1]), weight, preferred_element_type=f32
    ).astype(bf16)
    grad = head_major(grad_attn.reshape(queries.shape)).reshape(heads, q_tiles, tile_len, HEAD)

    attn = jnp.einsum("hqtl,hld->hqtd", probs_lo, val_e, preferred_element_type=f32)
    delta = jnp.sum(grad.astype(f32) * attn, axis=-1, keepdims=True)
    grad_probs = jnp.einsum("hqtd,hld->hqtl", grad, val_e, preferred_element_type=f32)
    grad_scores = (probs * (grad_probs - delta) * scale).astype(bf16)
    grad_q = jnp.einsum("hqtl,hld->hqtd", grad_scores, key_e, preferred_element_type=f32)
    grad_k = jnp.einsum("hqtl,hqtd->hld", grad_scores, query, preferred_element_type=f32)
    grad_v = jnp.einsum("hqtl,hqtd->hld", probs_lo, grad, preferred_element_type=f32)

    grad_q = grad_q.astype(bf16).reshape(heads, frames * tile_rows, tile_cols, tile_len, HEAD)
    shape_e = (heads, frames * ext_r, ext_c, tile_len, HEAD)
    own_k, own_v = folded(grad_k.reshape(shape_e), grad_v.reshape(shape_e))
    return (head_minor(grad_q), head_minor(own_k.astype(bf16)), head_minor(own_v.astype(bf16)))


def solution(mesh):
    in_specs = (
        P(None, "ha", "wa", None, "tp"),
        P(None, "ha", "wa", None, "tp"),
        P(None, "ha", "wa", None, "tp"),
        P(None, "ha", "wa", None, "tp"),
        P(("ha", "wa"), "tp"),
    )
    out_specs = (
        P(None, "ha", "wa", None, "tp"),
        P(None, "ha", "wa", None, "tp"),
        P(None, "ha", "wa", None, "tp"),
    )
    return jax.shard_map(local, mesh=mesh, in_specs=in_specs, out_specs=out_specs, check_vma=False)
```

```python
import jax
import jax.numpy as jnp
from jax import lax
from jax.sharding import PartitionSpec as P

HEAD = 128


def doubling_gather(block, steps):
    sizes = {"ha": lax.axis_size("ha"), "wa": lax.axis_size("wa")}
    index = {"ha": lax.axis_index("ha"), "wa": lax.axis_index("wa")}

    def swap(value, axis, bit):
        return lax.ppermute(value, axis, [(i, i ^ bit) for i in range(sizes[axis])])

    def low(axis, bit):
        return (index[axis] // bit) % 2 == 0

    def joined(axis, bit, mine, other):
        return jnp.where(low(axis, bit), jnp.concatenate([mine, other], 0), jnp.concatenate([other, mine], 0))

    buf = block
    for axis, bit in steps[:-2]:
        buf = joined(axis, bit, buf, swap(buf, axis, bit))
    (axis_a, bit_a), (axis_b, bit_b) = steps[-2:]
    across_a = swap(buf, axis_a, bit_a)
    across_b = swap(buf, axis_b, bit_b)
    diagonal = swap(across_a, axis_b, bit_b)
    near = joined(axis_a, bit_a, buf, across_a)
    far = joined(axis_a, bit_a, across_b, diagonal)
    return joined(axis_b, bit_b, near, far)


def gather_rows(out_proj):
    ha, wa = lax.axis_size("ha"), lax.axis_size("wa")
    ha_bits = [1 << b for b in range(ha.bit_length() - 1)]
    wa_bits = [1 << b for b in range(wa.bit_length() - 1)]
    steps = [("wa", b) for b in reversed(wa_bits)] + [("ha", b) for b in reversed(ha_bits)]
    buf = doubling_gather(out_proj, steps)
    rows, cols = out_proj.shape
    order = list(reversed(steps))
    buf = buf.reshape([2] * len(steps) + [rows, cols])
    natural = [("ha", b) for b in reversed(ha_bits)] + [("wa", b) for b in reversed(wa_bits)]
    perm = [order.index(s) for s in natural] + [len(steps), len(steps) + 1]
    return buf.transpose(perm).reshape(-1, cols)


def pick(length, d):
    if d < 0:
        return slice(length - 1, length)
    if d > 0:
        return slice(0, 1)
    return slice(0, length)


def neighbour_pairs(d_r, d_c):
    ha, wa = lax.axis_size("ha"), lax.axis_size("wa")
    pairs = []
    for i in range(ha):
        for j in range(wa):
            ti, tj = i - d_r, j - d_c
            if 0 <= ti < ha and 0 <= tj < wa:
                pairs.append((i * wa + j, ti * wa + tj))
    return pairs


DIRS = [(-1, -1), (-1, 0), (-1, 1), (0, -1), (0, 1), (1, -1), (1, 0), (1, 1)]


def extended(stacked):
    _, _, rows, cols = stacked.shape[:4]
    out = jnp.pad(stacked, ((0, 0), (0, 0), (1, 1), (1, 1), (0, 0), (0, 0)))
    for d_r, d_c in DIRS:
        piece = stacked[:, :, pick(rows, d_r), pick(cols, d_c)]
        got = lax.ppermute(piece, ("ha", "wa"), neighbour_pairs(d_r, d_c))
        r0 = 0 if d_r < 0 else (rows + 1 if d_r > 0 else 1)
        c0 = 0 if d_c < 0 else (cols + 1 if d_c > 0 else 1)
        out = lax.dynamic_update_slice(out, got, (0, 0, r0, c0, 0, 0))
    return out


def passed_along(value, axis, steps):
    count = lax.axis_size(axis)
    first, last = (max(0, -steps), min(count, count - steps))
    return lax.ppermute(value, axis, [(source, source + steps) for source in range(first, last)])


def sent_back(pieces, axis, steps):
    got = passed_along(jnp.stack(pieces).astype(jnp.bfloat16), axis, steps)
    return got.astype(jnp.float32)


def extended_2(array, sides, width):
    for axis, dim in sides:
        peers, length = (lax.axis_size(axis), array.shape[dim])
        up = [(i, (i + 1) % peers) for i in range(peers - 1)]
        down = [(j, i) for i, j in up]
        last = lax.slice_in_dim(array, length - width, length, axis=dim)
        first = lax.slice_in_dim(array, 0, width, axis=dim)
        before = lax.ppermute(last, axis, up)
        after = lax.ppermute(first, axis, down)
        array = jnp.concatenate([before, array, after], axis=dim)
    return array


def folded(grad_k, grad_v):
    from_below = sent_back([grad_k[:, 0], grad_v[:, 0]], "ha", -1)
    from_above = sent_back([grad_k[:, -1], grad_v[:, -1]], "ha", 1)
    own = []
    for n, part in enumerate((grad_k, grad_v)):
        inner = part[:, 1:-1]
        inner = inner.at[:, 0:1].add(from_above[n][:, None])
        inner = inner.at[:, -1:].add(from_below[n][:, None])
        own.append(inner)
    from_right = sent_back([own[0][:, :, 0], own[1][:, :, 0]], "wa", -1)
    from_left = sent_back([own[0][:, :, -1], own[1][:, :, -1]], "wa", 1)
    result = []
    for n, part in enumerate(own):
        inner = part[:, :, 1:-1]
        inner = inner.at[:, :, 0:1].add(from_left[n][:, :, None])
        inner = inner.at[:, :, -1:].add(from_right[n][:, :, None])
        result.append(inner)
    return result[0], result[1]


def local(queries, keys, values, grad_out, out_proj):
    frames, tile_rows, tile_cols, tile_len, columns = queries.shape
    heads = columns // HEAD
    f32, bf16 = jnp.float32, jnp.bfloat16
    whole = lax.all_gather(grad_out, "tp", axis=4, tiled=True)
    weight = gather_rows(out_proj)

    def head_major(array):
        split = array.reshape(frames * tile_rows, tile_cols, tile_len, heads, HEAD)
        return jnp.transpose(split, (3, 0, 1, 2, 4))

    def head_minor(array):
        return jnp.transpose(array, (1, 2, 3, 0, 4)).reshape(queries.shape)

    ext = extended_2(jnp.stack([head_major(keys), head_major(values)]), (("wa", 3), ("ha", 2)), 1)
    ext_r, ext_c = tile_rows + 2, tile_cols + 2
    row_base = lax.axis_index("ha") * tile_rows
    col_base = lax.axis_index("wa") * tile_cols
    rows_all = tile_rows * lax.axis_size("ha")
    cols_all = tile_cols * lax.axis_size("wa")
    qr = jnp.arange(tile_rows, dtype=jnp.int32)
    qc = jnp.arange(tile_cols, dtype=jnp.int32)
    sr = jnp.clip(row_base + qr - 1, 0, rows_all - 3) - row_base + 1
    sc = jnp.clip(col_base + qc - 1, 0, cols_all - 3) - col_base + 1
    kr = jnp.arange(ext_r, dtype=jnp.int32)
    kc = jnp.arange(ext_c, dtype=jnp.int32)
    in_r = (kr[None, :] >= sr[:, None]) & (kr[None, :] < sr[:, None] + 3)
    in_c = (kc[None, :] >= sc[:, None]) & (kc[None, :] < sc[:, None] + 3)
    inside = in_r[:, None, :, None] & in_c[None, :, None, :]
    inside = inside.reshape(tile_rows * tile_cols, 1, ext_r * ext_c, 1)
    inside = jnp.broadcast_to(inside, (tile_rows * tile_cols, 1, ext_r * ext_c, tile_len))
    inside = inside.reshape(1, tile_rows * tile_cols, 1, ext_r * ext_c * tile_len)
    q_tiles = tile_rows * tile_cols
    keys_n = ext_r * ext_c * tile_len
    scale = HEAD ** (-0.5)

    key_e = ext[0].reshape(heads, keys_n, HEAD)
    val_e = ext[1].reshape(heads, keys_n, HEAD)
    query = head_major(queries).reshape(heads, q_tiles, tile_len, HEAD)

    scores = jnp.einsum("hqtd,hld->hqtl", query, key_e, preferred_element_type=f32) * scale
    scores = jnp.where(inside, scores, -jnp.inf)
    scores = scores - jnp.max(scores, axis=-1, keepdims=True)
    expo = jnp.exp(scores)
    probs = expo / jnp.sum(expo, axis=-1, keepdims=True)
    probs_lo = probs.astype(bf16)

    grad_attn = jnp.dot(
        whole.reshape(-1, whole.shape[-1]), weight, preferred_element_type=f32
    ).astype(bf16)
    grad = head_major(grad_attn.reshape(queries.shape)).reshape(heads, q_tiles, tile_len, HEAD)

    attn = jnp.einsum("hqtl,hld->hqtd", probs_lo, val_e, preferred_element_type=f32)
    delta = jnp.sum(grad.astype(f32) * attn, axis=-1, keepdims=True)
    grad_probs = jnp.einsum("hqtd,hld->hqtl", grad, val_e, preferred_element_type=f32)
    grad_scores = (probs * (grad_probs - delta) * scale).astype(bf16)
    grad_q = jnp.einsum("hqtl,hld->hqtd", grad_scores, key_e, preferred_element_type=f32)
    grad_k = jnp.einsum("hqtl,hqtd->hld", grad_scores, query, preferred_element_type=f32)
    grad_v = jnp.einsum("hqtl,hqtd->hld", probs_lo, grad, preferred_element_type=f32)

    grad_q = grad_q.astype(bf16).reshape(heads, frames * tile_rows, tile_cols, tile_len, HEAD)
    shape_e = (heads, frames * ext_r, ext_c, tile_len, HEAD)
    own_k, own_v = folded(grad_k.reshape(shape_e), grad_v.reshape(shape_e))
    return (head_minor(grad_q), head_minor(own_k.astype(bf16)), head_minor(own_v.astype(bf16)))


def solution(mesh):
    in_specs = (
        P(None, "ha", "wa", None, "tp"),
        P(None, "ha", "wa", None, "tp"),
        P(None, "ha", "wa", None, "tp"),
        P(None, "ha", "wa", None, "tp"),
        P(("ha", "wa"), "tp"),
    )
    out_specs = (
        P(None, "ha", "wa", None, "tp"),
        P(None, "ha", "wa", None, "tp"),
        P(None, "ha", "wa", None, "tp"),
    )
    return jax.shard_map(local, mesh=mesh, in_specs=in_specs, out_specs=out_specs, check_vma=False)
```

```python
import jax
import jax.numpy as jnp
from jax import lax
from jax.sharding import PartitionSpec as P

HEAD = 128


def doubling_gather(block, steps):
    sizes = {"ha": lax.axis_size("ha"), "wa": lax.axis_size("wa")}
    index = {"ha": lax.axis_index("ha"), "wa": lax.axis_index("wa")}
    buf = block
    for axis, bit in steps:
        count = sizes[axis]
        other = lax.ppermute(buf, axis, [(i, i ^ bit) for i in range(count)])
        low = (index[axis] // bit) % 2 == 0
        buf = jnp.where(low, jnp.concatenate([buf, other], 0), jnp.concatenate([other, buf], 0))
    return buf


def gather_rows(out_proj):
    ha, wa = lax.axis_size("ha"), lax.axis_size("wa")
    ha_bits = [1 << b for b in range(ha.bit_length() - 1)]
    wa_bits = [1 << b for b in range(wa.bit_length() - 1)]
    steps = [("wa", b) for b in reversed(wa_bits)] + [("ha", b) for b in reversed(ha_bits)]
    steps = steps[:-2] + steps[-2:][::-1]
    buf = doubling_gather(out_proj, steps)
    rows, cols = out_proj.shape
    order = list(reversed(steps))
    buf = buf.reshape([2] * len(steps) + [rows, cols])
    natural = [("ha", b) for b in reversed(ha_bits)] + [("wa", b) for b in reversed(wa_bits)]
    perm = [order.index(s) for s in natural] + [len(steps), len(steps) + 1]
    return buf.transpose(perm).reshape(-1, cols)


def pick(length, d):
    if d < 0:
        return slice(length - 1, length)
    if d > 0:
        return slice(0, 1)
    return slice(0, length)


def neighbour_pairs(d_r, d_c):
    ha, wa = lax.axis_size("ha"), lax.axis_size("wa")
    pairs = []
    for i in range(ha):
        for j in range(wa):
            ti, tj = i - d_r, j - d_c
            if 0 <= ti < ha and 0 <= tj < wa:
                pairs.append((i * wa + j, ti * wa + tj))
    return pairs


DIRS = [(-1, -1), (-1, 0), (-1, 1), (0, -1), (0, 1), (1, -1), (1, 0), (1, 1)]


def extended(stacked):
    _, _, rows, cols = stacked.shape[:4]
    out = jnp.pad(stacked, ((0, 0), (0, 0), (1, 1), (1, 1), (0, 0), (0, 0)))
    for d_r, d_c in DIRS:
        piece = stacked[:, :, pick(rows, d_r), pick(cols, d_c)]
        got = lax.ppermute(piece, ("ha", "wa"), neighbour_pairs(d_r, d_c))
        r0 = 0 if d_r < 0 else (rows + 1 if d_r > 0 else 1)
        c0 = 0 if d_c < 0 else (cols + 1 if d_c > 0 else 1)
        out = lax.dynamic_update_slice(out, got, (0, 0, r0, c0, 0, 0))
    return out


def passed_along(value, axis, steps):
    count = lax.axis_size(axis)
    first, last = (max(0, -steps), min(count, count - steps))
    return lax.ppermute(value, axis, [(source, source + steps) for source in range(first, last)])


def sent_back(pieces, axis, steps):
    got = passed_along(jnp.stack(pieces).astype(jnp.bfloat16), axis, steps)
    return got.astype(jnp.float32)


def extended_2(array, sides, width):
    for axis, dim in sides:
        peers, length = (lax.axis_size(axis), array.shape[dim])
        up = [(i, (i + 1) % peers) for i in range(peers - 1)]
        down = [(j, i) for i, j in up]
        last = lax.slice_in_dim(array, length - width, length, axis=dim)
        first = lax.slice_in_dim(array, 0, width, axis=dim)
        before = lax.ppermute(last, axis, up)
        after = lax.ppermute(first, axis, down)
        array = jnp.concatenate([before, array, after], axis=dim)
    return array


def folded(grad_k, grad_v):
    from_below = sent_back([grad_k[:, 0], grad_v[:, 0]], "ha", -1)
    from_above = sent_back([grad_k[:, -1], grad_v[:, -1]], "ha", 1)
    own = []
    for n, part in enumerate((grad_k, grad_v)):
        inner = part[:, 1:-1]
        inner = inner.at[:, 0:1].add(from_above[n][:, None])
        inner = inner.at[:, -1:].add(from_below[n][:, None])
        own.append(inner)
    from_right = sent_back([own[0][:, :, 0], own[1][:, :, 0]], "wa", -1)
    from_left = sent_back([own[0][:, :, -1], own[1][:, :, -1]], "wa", 1)
    result = []
    for n, part in enumerate(own):
        inner = part[:, :, 1:-1]
        inner = inner.at[:, :, 0:1].add(from_left[n][:, :, None])
        inner = inner.at[:, :, -1:].add(from_right[n][:, :, None])
        result.append(inner)
    return result[0], result[1]


def local(queries, keys, values, grad_out, out_proj):
    frames, tile_rows, tile_cols, tile_len, columns = queries.shape
    heads = columns // HEAD
    f32, bf16 = jnp.float32, jnp.bfloat16
    whole = lax.all_gather(grad_out, "tp", axis=4, tiled=True)
    weight = gather_rows(out_proj)

    def head_major(array):
        split = array.reshape(frames * tile_rows, tile_cols, tile_len, heads, HEAD)
        return jnp.transpose(split, (3, 0, 1, 2, 4))

    def head_minor(array):
        return jnp.transpose(array, (1, 2, 3, 0, 4)).reshape(queries.shape)

    ext = extended_2(jnp.stack([head_major(keys), head_major(values)]), (("wa", 3), ("ha", 2)), 1)
    ext_r, ext_c = tile_rows + 2, tile_cols + 2
    row_base = lax.axis_index("ha") * tile_rows
    col_base = lax.axis_index("wa") * tile_cols
    rows_all = tile_rows * lax.axis_size("ha")
    cols_all = tile_cols * lax.axis_size("wa")
    qr = jnp.arange(tile_rows, dtype=jnp.int32)
    qc = jnp.arange(tile_cols, dtype=jnp.int32)
    sr = jnp.clip(row_base + qr - 1, 0, rows_all - 3) - row_base + 1
    sc = jnp.clip(col_base + qc - 1, 0, cols_all - 3) - col_base + 1
    kr = jnp.arange(ext_r, dtype=jnp.int32)
    kc = jnp.arange(ext_c, dtype=jnp.int32)
    in_r = (kr[None, :] >= sr[:, None]) & (kr[None, :] < sr[:, None] + 3)
    in_c = (kc[None, :] >= sc[:, None]) & (kc[None, :] < sc[:, None] + 3)
    inside = in_r[:, None, :, None] & in_c[None, :, None, :]
    inside = inside.reshape(tile_rows * tile_cols, 1, ext_r * ext_c, 1)
    inside = jnp.broadcast_to(inside, (tile_rows * tile_cols, 1, ext_r * ext_c, tile_len))
    inside = inside.reshape(1, tile_rows * tile_cols, 1, ext_r * ext_c * tile_len)
    q_tiles = tile_rows * tile_cols
    keys_n = ext_r * ext_c * tile_len
    scale = HEAD ** (-0.5)

    key_e = ext[0].reshape(heads, keys_n, HEAD)
    val_e = ext[1].reshape(heads, keys_n, HEAD)
    query = head_major(queries).reshape(heads, q_tiles, tile_len, HEAD)

    scores = jnp.einsum("hqtd,hld->hqtl", query, key_e, preferred_element_type=f32) * scale
    scores = jnp.where(inside, scores, -jnp.inf)
    scores = scores - jnp.max(scores, axis=-1, keepdims=True)
    expo = jnp.exp(scores)
    probs = expo / jnp.sum(expo, axis=-1, keepdims=True)
    probs_lo = probs.astype(bf16)

    grad_attn = jnp.dot(
        whole.reshape(-1, whole.shape[-1]), weight, preferred_element_type=f32
    ).astype(bf16)
    grad = head_major(grad_attn.reshape(queries.shape)).reshape(heads, q_tiles, tile_len, HEAD)

    attn = jnp.einsum("hqtl,hld->hqtd", probs_lo, val_e, preferred_element_type=f32)
    delta = jnp.sum(grad.astype(f32) * attn, axis=-1, keepdims=True)
    grad_probs = jnp.einsum("hqtd,hld->hqtl", grad, val_e, preferred_element_type=f32)
    grad_scores = (probs * (grad_probs - delta) * scale).astype(bf16)
    grad_q = jnp.einsum("hqtl,hld->hqtd", grad_scores, key_e, preferred_element_type=f32)
    grad_k = jnp.einsum("hqtl,hqtd->hld", grad_scores, query, preferred_element_type=f32)
    grad_v = jnp.einsum("hqtl,hqtd->hld", probs_lo, grad, preferred_element_type=f32)

    grad_q = grad_q.astype(bf16).reshape(heads, frames * tile_rows, tile_cols, tile_len, HEAD)
    shape_e = (heads, frames * ext_r, ext_c, tile_len, HEAD)
    own_k, own_v = folded(grad_k.reshape(shape_e), grad_v.reshape(shape_e))
    return (head_minor(grad_q), head_minor(own_k.astype(bf16)), head_minor(own_v.astype(bf16)))


def solution(mesh):
    in_specs = (
        P(None, "ha", "wa", None, "tp"),
        P(None, "ha", "wa", None, "tp"),
        P(None, "ha", "wa", None, "tp"),
        P(None, "ha", "wa", None, "tp"),
        P(("ha", "wa"), "tp"),
    )
    out_specs = (
        P(None, "ha", "wa", None, "tp"),
        P(None, "ha", "wa", None, "tp"),
        P(None, "ha", "wa", None, "tp"),
    )
    return jax.shard_map(local, mesh=mesh, in_specs=in_specs, out_specs=out_specs, check_vma=False)
```

```python
import jax
import jax.numpy as jnp
from jax import lax
from jax.sharding import PartitionSpec as P

HEAD = 128


def doubling_gather(block, steps):
    sizes = {"ha": lax.axis_size("ha"), "wa": lax.axis_size("wa")}
    index = {"ha": lax.axis_index("ha"), "wa": lax.axis_index("wa")}
    buf = block
    for axis, bit in steps:
        count = sizes[axis]
        other = lax.ppermute(buf, axis, [(i, i ^ bit) for i in range(count)])
        low = (index[axis] // bit) % 2 == 0
        buf = jnp.where(low, jnp.concatenate([buf, other], 0), jnp.concatenate([other, buf], 0))
    return buf


def gather_rows(out_proj):
    ha, wa = lax.axis_size("ha"), lax.axis_size("wa")
    ha_bits = [1 << b for b in range(ha.bit_length() - 1)]
    wa_bits = [1 << b for b in range(wa.bit_length() - 1)]
    steps = [("wa", b) for b in wa_bits] + [("ha", b) for b in reversed(ha_bits)]
    buf = doubling_gather(out_proj, steps)
    rows, cols = out_proj.shape
    order = list(reversed(steps))
    buf = buf.reshape([2] * len(steps) + [rows, cols])
    natural = [("ha", b) for b in reversed(ha_bits)] + [("wa", b) for b in reversed(wa_bits)]
    perm = [order.index(s) for s in natural] + [len(steps), len(steps) + 1]
    return buf.transpose(perm).reshape(-1, cols)


def pick(length, d):
    if d < 0:
        return slice(length - 1, length)
    if d > 0:
        return slice(0, 1)
    return slice(0, length)


def neighbour_pairs(d_r, d_c):
    ha, wa = lax.axis_size("ha"), lax.axis_size("wa")
    pairs = []
    for i in range(ha):
        for j in range(wa):
            ti, tj = i - d_r, j - d_c
            if 0 <= ti < ha and 0 <= tj < wa:
                pairs.append((i * wa + j, ti * wa + tj))
    return pairs


DIRS = [(-1, -1), (-1, 0), (-1, 1), (0, -1), (0, 1), (1, -1), (1, 0), (1, 1)]


def extended(stacked):
    _, _, rows, cols = stacked.shape[:4]
    out = jnp.pad(stacked, ((0, 0), (0, 0), (1, 1), (1, 1), (0, 0), (0, 0)))
    for d_r, d_c in DIRS:
        piece = stacked[:, :, pick(rows, d_r), pick(cols, d_c)]
        got = lax.ppermute(piece, ("ha", "wa"), neighbour_pairs(d_r, d_c))
        r0 = 0 if d_r < 0 else (rows + 1 if d_r > 0 else 1)
        c0 = 0 if d_c < 0 else (cols + 1 if d_c > 0 else 1)
        out = lax.dynamic_update_slice(out, got, (0, 0, r0, c0, 0, 0))
    return out


def passed_along(value, axis, steps):
    count = lax.axis_size(axis)
    first, last = (max(0, -steps), min(count, count - steps))
    return lax.ppermute(value, axis, [(source, source + steps) for source in range(first, last)])


def sent_back(pieces, axis, steps):
    got = passed_along(jnp.stack(pieces).astype(jnp.bfloat16), axis, steps)
    return got.astype(jnp.float32)


def extended_2(array, sides, width):
    for axis, dim in sides:
        peers, length = (lax.axis_size(axis), array.shape[dim])
        up = [(i, (i + 1) % peers) for i in range(peers - 1)]
        down = [(j, i) for i, j in up]
        last = lax.slice_in_dim(array, length - width, length, axis=dim)
        first = lax.slice_in_dim(array, 0, width, axis=dim)
        before = lax.ppermute(last, axis, up)
        after = lax.ppermute(first, axis, down)
        array = jnp.concatenate([before, array, after], axis=dim)
    return array


def folded(grad_k, grad_v):
    from_below = sent_back([grad_k[:, 0], grad_v[:, 0]], "ha", -1)
    from_above = sent_back([grad_k[:, -1], grad_v[:, -1]], "ha", 1)
    own = []
    for n, part in enumerate((grad_k, grad_v)):
        inner = part[:, 1:-1]
        inner = inner.at[:, 0:1].add(from_above[n][:, None])
        inner = inner.at[:, -1:].add(from_below[n][:, None])
        own.append(inner)
    from_right = sent_back([own[0][:, :, 0], own[1][:, :, 0]], "wa", -1)
    from_left = sent_back([own[0][:, :, -1], own[1][:, :, -1]], "wa", 1)
    result = []
    for n, part in enumerate(own):
        inner = part[:, :, 1:-1]
        inner = inner.at[:, :, 0:1].add(from_left[n][:, :, None])
        inner = inner.at[:, :, -1:].add(from_right[n][:, :, None])
        result.append(inner)
    return result[0], result[1]


def local(queries, keys, values, grad_out, out_proj):
    frames, tile_rows, tile_cols, tile_len, columns = queries.shape
    heads = columns // HEAD
    f32, bf16 = jnp.float32, jnp.bfloat16
    whole = lax.all_gather(grad_out, "tp", axis=4, tiled=True)
    weight = gather_rows(out_proj)

    def head_major(array):
        split = array.reshape(frames * tile_rows, tile_cols, tile_len, heads, HEAD)
        return jnp.transpose(split, (3, 0, 1, 2, 4))

    def head_minor(array):
        return jnp.transpose(array, (1, 2, 3, 0, 4)).reshape(queries.shape)

    ext = extended_2(jnp.stack([head_major(keys), head_major(values)]), (("wa", 3), ("ha", 2)), 1)
    ext_r, ext_c = tile_rows + 2, tile_cols + 2
    row_base = lax.axis_index("ha") * tile_rows
    col_base = lax.axis_index("wa") * tile_cols
    rows_all = tile_rows * lax.axis_size("ha")
    cols_all = tile_cols * lax.axis_size("wa")
    qr = jnp.arange(tile_rows, dtype=jnp.int32)
    qc = jnp.arange(tile_cols, dtype=jnp.int32)
    sr = jnp.clip(row_base + qr - 1, 0, rows_all - 3) - row_base + 1
    sc = jnp.clip(col_base + qc - 1, 0, cols_all - 3) - col_base + 1
    kr = jnp.arange(ext_r, dtype=jnp.int32)
    kc = jnp.arange(ext_c, dtype=jnp.int32)
    in_r = (kr[None, :] >= sr[:, None]) & (kr[None, :] < sr[:, None] + 3)
    in_c = (kc[None, :] >= sc[:, None]) & (kc[None, :] < sc[:, None] + 3)
    inside = in_r[:, None, :, None] & in_c[None, :, None, :]
    inside = inside.reshape(tile_rows * tile_cols, 1, ext_r * ext_c, 1)
    inside = jnp.broadcast_to(inside, (tile_rows * tile_cols, 1, ext_r * ext_c, tile_len))
    inside = inside.reshape(1, tile_rows * tile_cols, 1, ext_r * ext_c * tile_len)
    q_tiles = tile_rows * tile_cols
    keys_n = ext_r * ext_c * tile_len
    scale = HEAD ** (-0.5)

    key_e = ext[0].reshape(heads, keys_n, HEAD)
    val_e = ext[1].reshape(heads, keys_n, HEAD)
    query = head_major(queries).reshape(heads, q_tiles, tile_len, HEAD)

    scores = jnp.einsum("hqtd,hld->hqtl", query, key_e, preferred_element_type=f32) * scale
    scores = jnp.where(inside, scores, -jnp.inf)
    scores = scores - jnp.max(scores, axis=-1, keepdims=True)
    expo = jnp.exp(scores)
    probs = expo / jnp.sum(expo, axis=-1, keepdims=True)
    probs_lo = probs.astype(bf16)

    grad_attn = jnp.dot(
        whole.reshape(-1, whole.shape[-1]), weight, preferred_element_type=f32
    ).astype(bf16)
    grad = head_major(grad_attn.reshape(queries.shape)).reshape(heads, q_tiles, tile_len, HEAD)

    attn = jnp.einsum("hqtl,hld->hqtd", probs_lo, val_e, preferred_element_type=f32)
    delta = jnp.sum(grad.astype(f32) * attn, axis=-1, keepdims=True)
    grad_probs = jnp.einsum("hqtd,hld->hqtl", grad, val_e, preferred_element_type=f32)
    grad_scores = (probs * (grad_probs - delta) * scale).astype(bf16)
    grad_q = jnp.einsum("hqtl,hld->hqtd", grad_scores, key_e, preferred_element_type=f32)
    grad_k = jnp.einsum("hqtl,hqtd->hld", grad_scores, query, preferred_element_type=f32)
    grad_v = jnp.einsum("hqtl,hqtd->hld", probs_lo, grad, preferred_element_type=f32)

    grad_q = grad_q.astype(bf16).reshape(heads, frames * tile_rows, tile_cols, tile_len, HEAD)
    shape_e = (heads, frames * ext_r, ext_c, tile_len, HEAD)
    own_k, own_v = folded(grad_k.reshape(shape_e), grad_v.reshape(shape_e))
    return (head_minor(grad_q), head_minor(own_k.astype(bf16)), head_minor(own_v.astype(bf16)))


def solution(mesh):
    in_specs = (
        P(None, "ha", "wa", None, "tp"),
        P(None, "ha", "wa", None, "tp"),
        P(None, "ha", "wa", None, "tp"),
        P(None, "ha", "wa", None, "tp"),
        P(("ha", "wa"), "tp"),
    )
    out_specs = (
        P(None, "ha", "wa", None, "tp"),
        P(None, "ha", "wa", None, "tp"),
        P(None, "ha", "wa", None, "tp"),
    )
    return jax.shard_map(local, mesh=mesh, in_specs=in_specs, out_specs=out_specs, check_vma=False)
```

```python
import jax
import jax.numpy as jnp
from jax import lax
from jax.sharding import PartitionSpec as P

HEAD = 128


def doubling_gather(block, steps):
    sizes = {"ha": lax.axis_size("ha"), "wa": lax.axis_size("wa")}
    index = {"ha": lax.axis_index("ha"), "wa": lax.axis_index("wa")}
    buf = block
    for axis, bit in steps:
        count = sizes[axis]
        other = lax.ppermute(buf, axis, [(i, i ^ bit) for i in range(count)])
        low = (index[axis] // bit) % 2 == 0
        buf = jnp.where(low, jnp.concatenate([buf, other], 0), jnp.concatenate([other, buf], 0))
    return buf


def gather_rows(out_proj):
    ha, wa = lax.axis_size("ha"), lax.axis_size("wa")
    ha_bits = [1 << b for b in range(ha.bit_length() - 1)]
    wa_bits = [1 << b for b in range(wa.bit_length() - 1)]
    steps = [("wa", b) for b in reversed(wa_bits)] + [("ha", b) for b in reversed(ha_bits)]
    steps = [steps[0], steps[2], steps[1]] + steps[3:]
    buf = doubling_gather(out_proj, steps)
    rows, cols = out_proj.shape
    order = list(reversed(steps))
    buf = buf.reshape([2] * len(steps) + [rows, cols])
    natural = [("ha", b) for b in reversed(ha_bits)] + [("wa", b) for b in reversed(wa_bits)]
    perm = [order.index(s) for s in natural] + [len(steps), len(steps) + 1]
    return buf.transpose(perm).reshape(-1, cols)


def pick(length, d):
    if d < 0:
        return slice(length - 1, length)
    if d > 0:
        return slice(0, 1)
    return slice(0, length)


def neighbour_pairs(d_r, d_c):
    ha, wa = lax.axis_size("ha"), lax.axis_size("wa")
    pairs = []
    for i in range(ha):
        for j in range(wa):
            ti, tj = i - d_r, j - d_c
            if 0 <= ti < ha and 0 <= tj < wa:
                pairs.append((i * wa + j, ti * wa + tj))
    return pairs


DIRS = [(-1, -1), (-1, 0), (-1, 1), (0, -1), (0, 1), (1, -1), (1, 0), (1, 1)]


def extended(stacked):
    _, _, rows, cols = stacked.shape[:4]
    out = jnp.pad(stacked, ((0, 0), (0, 0), (1, 1), (1, 1), (0, 0), (0, 0)))
    for d_r, d_c in DIRS:
        piece = stacked[:, :, pick(rows, d_r), pick(cols, d_c)]
        got = lax.ppermute(piece, ("ha", "wa"), neighbour_pairs(d_r, d_c))
        r0 = 0 if d_r < 0 else (rows + 1 if d_r > 0 else 1)
        c0 = 0 if d_c < 0 else (cols + 1 if d_c > 0 else 1)
        out = lax.dynamic_update_slice(out, got, (0, 0, r0, c0, 0, 0))
    return out


def passed_along(value, axis, steps):
    count = lax.axis_size(axis)
    first, last = (max(0, -steps), min(count, count - steps))
    return lax.ppermute(value, axis, [(source, source + steps) for source in range(first, last)])


def sent_back(pieces, axis, steps):
    got = passed_along(jnp.stack(pieces).astype(jnp.bfloat16), axis, steps)
    return got.astype(jnp.float32)


def extended_2(array, sides, width):
    for axis, dim in sides:
        peers, length = (lax.axis_size(axis), array.shape[dim])
        up = [(i, (i + 1) % peers) for i in range(peers - 1)]
        down = [(j, i) for i, j in up]
        last = lax.slice_in_dim(array, length - width, length, axis=dim)
        first = lax.slice_in_dim(array, 0, width, axis=dim)
        before = lax.ppermute(last, axis, up)
        after = lax.ppermute(first, axis, down)
        array = jnp.concatenate([before, array, after], axis=dim)
    return array


def folded(grad_k, grad_v):
    from_below = sent_back([grad_k[:, 0], grad_v[:, 0]], "ha", -1)
    from_above = sent_back([grad_k[:, -1], grad_v[:, -1]], "ha", 1)
    own = []
    for n, part in enumerate((grad_k, grad_v)):
        inner = part[:, 1:-1]
        inner = inner.at[:, 0:1].add(from_above[n][:, None])
        inner = inner.at[:, -1:].add(from_below[n][:, None])
        own.append(inner)
    from_right = sent_back([own[0][:, :, 0], own[1][:, :, 0]], "wa", -1)
    from_left = sent_back([own[0][:, :, -1], own[1][:, :, -1]], "wa", 1)
    result = []
    for n, part in enumerate(own):
        inner = part[:, :, 1:-1]
        inner = inner.at[:, :, 0:1].add(from_left[n][:, :, None])
        inner = inner.at[:, :, -1:].add(from_right[n][:, :, None])
        result.append(inner)
    return result[0], result[1]


def local(queries, keys, values, grad_out, out_proj):
    frames, tile_rows, tile_cols, tile_len, columns = queries.shape
    heads = columns // HEAD
    f32, bf16 = jnp.float32, jnp.bfloat16
    whole = lax.all_gather(grad_out, "tp", axis=4, tiled=True)
    weight = gather_rows(out_proj)

    def head_major(array):
        split = array.reshape(frames * tile_rows, tile_cols, tile_len, heads, HEAD)
        return jnp.transpose(split, (3, 0, 1, 2, 4))

    def head_minor(array):
        return jnp.transpose(array, (1, 2, 3, 0, 4)).reshape(queries.shape)

    ext = extended_2(jnp.stack([head_major(keys), head_major(values)]), (("wa", 3), ("ha", 2)), 1)
    ext_r, ext_c = tile_rows + 2, tile_cols + 2
    row_base = lax.axis_index("ha") * tile_rows
    col_base = lax.axis_index("wa") * tile_cols
    rows_all = tile_rows * lax.axis_size("ha")
    cols_all = tile_cols * lax.axis_size("wa")
    qr = jnp.arange(tile_rows, dtype=jnp.int32)
    qc = jnp.arange(tile_cols, dtype=jnp.int32)
    sr = jnp.clip(row_base + qr - 1, 0, rows_all - 3) - row_base + 1
    sc = jnp.clip(col_base + qc - 1, 0, cols_all - 3) - col_base + 1
    kr = jnp.arange(ext_r, dtype=jnp.int32)
    kc = jnp.arange(ext_c, dtype=jnp.int32)
    in_r = (kr[None, :] >= sr[:, None]) & (kr[None, :] < sr[:, None] + 3)
    in_c = (kc[None, :] >= sc[:, None]) & (kc[None, :] < sc[:, None] + 3)
    inside = in_r[:, None, :, None] & in_c[None, :, None, :]
    inside = inside.reshape(tile_rows * tile_cols, 1, ext_r * ext_c, 1)
    inside = jnp.broadcast_to(inside, (tile_rows * tile_cols, 1, ext_r * ext_c, tile_len))
    inside = inside.reshape(1, tile_rows * tile_cols, 1, ext_r * ext_c * tile_len)
    q_tiles = tile_rows * tile_cols
    keys_n = ext_r * ext_c * tile_len
    scale = HEAD ** (-0.5)

    key_e = ext[0].reshape(heads, keys_n, HEAD)
    val_e = ext[1].reshape(heads, keys_n, HEAD)
    query = head_major(queries).reshape(heads, q_tiles, tile_len, HEAD)

    scores = jnp.einsum("hqtd,hld->hqtl", query, key_e, preferred_element_type=f32) * scale
    scores = jnp.where(inside, scores, -jnp.inf)
    scores = scores - jnp.max(scores, axis=-1, keepdims=True)
    expo = jnp.exp(scores)
    probs = expo / jnp.sum(expo, axis=-1, keepdims=True)
    probs_lo = probs.astype(bf16)

    grad_attn = jnp.dot(
        whole.reshape(-1, whole.shape[-1]), weight, preferred_element_type=f32
    ).astype(bf16)
    grad = head_major(grad_attn.reshape(queries.shape)).reshape(heads, q_tiles, tile_len, HEAD)

    attn = jnp.einsum("hqtl,hld->hqtd", probs_lo, val_e, preferred_element_type=f32)
    delta = jnp.sum(grad.astype(f32) * attn, axis=-1, keepdims=True)
    grad_probs = jnp.einsum("hqtd,hld->hqtl", grad, val_e, preferred_element_type=f32)
    grad_scores = (probs * (grad_probs - delta) * scale).astype(bf16)
    grad_q = jnp.einsum("hqtl,hld->hqtd", grad_scores, key_e, preferred_element_type=f32)
    grad_k = jnp.einsum("hqtl,hqtd->hld", grad_scores, query, preferred_element_type=f32)
    grad_v = jnp.einsum("hqtl,hqtd->hld", probs_lo, grad, preferred_element_type=f32)

    grad_q = grad_q.astype(bf16).reshape(heads, frames * tile_rows, tile_cols, tile_len, HEAD)
    shape_e = (heads, frames * ext_r, ext_c, tile_len, HEAD)
    own_k, own_v = folded(grad_k.reshape(shape_e), grad_v.reshape(shape_e))
    return (head_minor(grad_q), head_minor(own_k.astype(bf16)), head_minor(own_v.astype(bf16)))


def solution(mesh):
    in_specs = (
        P(None, "ha", "wa", None, "tp"),
        P(None, "ha", "wa", None, "tp"),
        P(None, "ha", "wa", None, "tp"),
        P(None, "ha", "wa", None, "tp"),
        P(("ha", "wa"), "tp"),
    )
    out_specs = (
        P(None, "ha", "wa", None, "tp"),
        P(None, "ha", "wa", None, "tp"),
        P(None, "ha", "wa", None, "tp"),
    )
    return jax.shard_map(local, mesh=mesh, in_specs=in_specs, out_specs=out_specs, check_vma=False)
```
